32 devices in a mesh: dp: 4 (over y, core), fsdp: 8 (over z, x).
Axes of the slice: x: 2, y: 2, z: 4, core: 2. Of those that a mesh axis runs over, the one named last changes fastest.
Arguments:
- tokens: bfloat16 [32, 1024, 1024], P(('dp', 'fsdp')), may hold values from -6 to 6
- lengths: int32 [32], P(('dp', 'fsdp')), may hold values from 256 to 1024, as said below
- attend_weight: bfloat16 [1024, 3072], P(('dp', 'fsdp')), may hold values from -0.1875 to 0.1875
- project_weight: bfloat16 [1024, 1024], P(('dp', 'fsdp')), may hold values from -0.75 to 0.75
- expand_weight: bfloat16 [1024, 4096], P(('dp', 'fsdp')), may hold values from -0.1875 to 0.1875
- contract_weight: bfloat16 [4096, 1024], P(('dp', 'fsdp')), may hold values from -0.09375 to 0.09375
- inner_bias: bfloat16 [4096], P(('dp', 'fsdp')), may hold values from -3 to 3
- outer_bias: bfloat16 [1024], P(('dp', 'fsdp')), may hold values from -3 to 3
- norm_gain: bfloat16 [1024], P(('dp', 'fsdp')), may hold values from 0.25 to 1.75
- norm_shift: bfloat16 [1024], P(('dp', 'fsdp')), may hold values from -2 to 2
- cotangent: bfloat16 [32, 1024, 1024], P(('dp', 'fsdp')), may hold values from -6 to 6
Outputs:
- output: bfloat16 [32, 1024, 1024], P(('dp', 'fsdp'))
- grad_tokens: bfloat16 [32, 1024, 1024], P(('dp', 'fsdp'))
- grad_attend: float32 [1024, 3072], P(('dp', 'fsdp'))
- grad_project: float32 [1024, 1024], P(('dp', 'fsdp'))
- grad_expand: float32 [1024, 4096], P(('dp', 'fsdp'))
- grad_contract: float32 [4096, 1024], P(('dp', 'fsdp'))
- grad_inner: float32 [4096], P(('dp', 'fsdp'))
- grad_outer: float32 [1024], P(('dp', 'fsdp'))
- grad_gain: float32 [1024], P(('dp', 'fsdp'))
- grad_shift: float32 [1024], P(('dp', 'fsdp'))
The draws below stay inside these ranges and needn't reach their ends.
Inputs may be any that keep to these rules, and one draw needn't show every extreme that they name: rows 2i and 2i+1 have equal lengths; positions at or past a row's length are padding.
All inputs are finite; a program needn't handle non-finite values.
Results may differ from the reference program's by a relative error of at most 0.0085.
Values may be sent and summed in bfloat16 or wider, within the bound.
No kernel may reach another device: no remote copies, remote signals or barrier semaphores. Data moves between devices by JAX's collectives and lax.ppermute only.
A program may use at most 320 MiB of HBM per device.

```python
import math
import jax
import jax.numpy as jnp
from jax import lax

D = 1024
FF = 4096
HEADS = 16
HEAD_DIM = 64
ROT = 32
SEQ = 1024
SEQS = 32


def draw_lengths(key, part):
    pairs = SEQS // 2
    base = jax.random.randint(jax.random.fold_in(key, 11), (pairs,), SEQ // 4, SEQ + 1)
    order = jax.random.permutation(jax.random.fold_in(key, 12), pairs)
    base = base.at[order[0]].set(SEQ).at[order[1]].set(SEQ // 4)
    return jnp.repeat(base, 2).astype(jnp.int32)


def block_levels(stream_key, shape, pieces, least, largest):
    def one(dim, blocks):
        heights = jax.random.uniform(jax.random.fold_in(jax.random.fold_in(stream_key, 6), dim), (blocks,), jnp.float32, least / len(pieces), largest / len(pieces))
        return jnp.repeat(jnp.exp(heights), shape[dim] // blocks).reshape((-1,) + (1,) * (len(shape) - dim - 1))

    level = one(*pieces[0])
    for cut in pieces[1:]:
        level = level * one(*cut)
    return level


def bell_draw(stream_key, shape, deviation, bound, pieces=(), dtype=jnp.bfloat16):
    level = block_levels(stream_key, shape, pieces, -0.22, 0.18) if pieces else 1.0
    values = jax.random.normal(stream_key, shape, jnp.float32) * deviation * level
    return jnp.minimum(jnp.maximum(values, -bound), bound).astype(dtype)


def setup_inputs(seed: int = 0) -> dict:
    key_list = jax.random.split(jax.random.key(seed), 12)
    return {
        "tokens": bell_draw(key_list[0], (SEQS, SEQ, D), 1.0, 6.0, ((0, 32),)),
        "lengths": draw_lengths(jax.random.fold_in(key_list[11], 71), 0),
        "attend_weight": bell_draw(key_list[2], (D, 3 * D), D ** -0.5, 0.1875, ((0, 32),)),
        "project_weight": bell_draw(key_list[3], (D, D), (D // 16) ** -0.5, 0.75, ((0, 32),)),
        "expand_weight": bell_draw(key_list[4], (D, FF), D ** -0.5, 0.1875, ((0, 32),)),
        "contract_weight": bell_draw(key_list[5], (FF, D), FF ** -0.5, 0.09375, ((0, 32),)),
        "inner_bias": bell_draw(key_list[6], (FF,), 0.5, 3.0, ((0, 32),)),
        "outer_bias": bell_draw(key_list[7], (D,), 0.5, 3.0, ((0, 32),)),
        "norm_gain": jnp.clip(1.0 + 0.15 * jax.random.normal(key_list[8], (D,), jnp.float32), 0.25, 1.75).astype(jnp.bfloat16),
        "norm_shift": bell_draw(key_list[9], (D,), 0.3, 2.0, ((0, 32),)),
        "cotangent": bell_draw(key_list[10], (SEQS, SEQ, D), 1.0, 6.0, ((0, 32),)),
    }


highest = lax.Precision.HIGHEST
epsilon = 1e-05

@jax.custom_vjp
def low(v):
    return lax.optimization_barrier(v.astype(jnp.bfloat16)).astype(jnp.float32)

@jax.custom_vjp
def low_back(v):
    return v

def low_keep(v):
    return (low(v), None)

def low_pass(kept, grad):
    return (grad,)

def back_keep(v):
    return (v, None)

def back_low(kept, grad):
    return (low(grad),)
low.defvjp(low_keep, low_pass)
low_back.defvjp(back_keep, back_low)

def product(left, right):
    return jnp.dot(left, right, precision=highest, preferred_element_type=jnp.float32)

def layer_norm(rows, gain, shift):
    center = lax.optimization_barrier(jnp.mean(rows, axis=-1, keepdims=True))
    spread = rows - center
    variance = lax.optimization_barrier(jnp.mean(spread * spread, axis=-1, keepdims=True))
    return spread * lax.rsqrt(variance + epsilon) * gain + shift

def rotary_tables(length):
    position = jnp.arange(length).astype(jnp.float32)[:, None]
    ladder = jnp.arange(ROT // 2).astype(jnp.float32) * (-2.0 * math.log(10000.0) / ROT)
    angle = position * jnp.exp(ladder)[None, :]
    return (jnp.cos(angle)[:, None, :], jnp.sin(angle)[:, None, :])

def rotate(field, cosine, sine):
    paired = field[..., :ROT].reshape(field.shape[:-1] + (ROT // 2, 2))
    first = paired[..., 0]
    second = paired[..., 1]
    turned = jnp.stack([first * cosine - second * sine, second * cosine + first * sine], axis=-1)
    return jnp.concatenate([turned.reshape(field.shape[:-1] + (ROT,)), field[..., ROT:]], axis=-1)

def attend_one(query, keys, values, length):
    raw = jnp.einsum('qhd,khd->hqk', query, keys, precision=highest)
    scores = low_back(raw * HEAD_DIM ** (-0.5))
    places = jnp.arange(SEQ)
    allowed = (places[None, :] <= places[:, None]) & (places[None, :] < length)
    masked = jnp.where(allowed[None], scores, -1000000000.0)
    top = lax.optimization_barrier(jnp.max(masked, axis=-1, keepdims=True))
    weights = jnp.exp(masked - top)
    probs = low(weights / lax.optimization_barrier(jnp.sum(weights, axis=-1, keepdims=True)))
    return jnp.einsum('hqk,khd->qhd', probs, values, precision=highest)

def layer(block_rows, lengths, params):
    attend_weight, project_weight, expand_weight, contract_weight, inner_bias, outer_bias, norm_gain, norm_shift = params
    group = block_rows.shape[0]
    rows = block_rows.reshape(group * SEQ, D)
    normed = low(layer_norm(rows, norm_gain, norm_shift))
    triple = low_back(product(normed, attend_weight)).reshape(group, SEQ, 3, HEADS, HEAD_DIM)
    cosine, sine = rotary_tables(SEQ)
    query = low(rotate(triple[:, :, 0], cosine, sine))
    keys = low(rotate(triple[:, :, 1], cosine, sine))
    values = low(triple[:, :, 2])
    saved = jax.checkpoint(attend_one)
    attended = lax.map(lambda item: saved(item[0], item[1], item[2], item[3]), (query, keys, values, lengths))
    mixed = low(low_back(attended.reshape(group * SEQ, D)))
    hidden = low_back(product(normed, expand_weight) + inner_bias)
    active = low(jax.nn.gelu(hidden, approximate=True))
    result = rows + product(mixed, project_weight) + product(active, contract_weight) + outer_bias
    return result.reshape(group, SEQ, D)

def reference(tokens, lengths, attend_weight, project_weight, expand_weight, contract_weight, inner_bias, outer_bias, norm_gain, norm_shift, cotangent):
    params = (attend_weight, project_weight, expand_weight, contract_weight, inner_bias, outer_bias, norm_gain, norm_shift)
    params = tuple((item.astype(jnp.float32) for item in params))
    per_group = math.gcd(SEQS, max(1, 4096 // SEQ))
    groups = SEQS // per_group
    token_groups = tokens.astype(jnp.float32).reshape(groups, per_group, SEQ, D)
    length_groups = lengths.reshape(groups, per_group)
    grad_groups = cotangent.astype(jnp.float32).reshape(groups, per_group, SEQ, D)

    def one_group(totals, item):
        block_rows, block_lengths, block_grad = item
        result, pull = jax.vjp(lambda inputs, weights: layer(inputs, block_lengths, weights), block_rows, params)
        input_grad, param_grad = pull(block_grad)
        totals = jax.tree.map(jnp.add, totals, param_grad)
        return (totals, (result.astype(jnp.bfloat16), input_grad.astype(jnp.bfloat16)))
    zeros = tuple((jnp.zeros(item.shape, jnp.float32) for item in params))
    totals, (results, input_grads) = lax.scan(one_group, zeros, (token_groups, length_groups, grad_groups))
    output = results.reshape(SEQS, SEQ, D)
    grad_tokens = input_grads.reshape(SEQS, SEQ, D)
    return (output, grad_tokens, totals[0], totals[1], totals[2], totals[3], totals[4], totals[5], totals[6], totals[7])
```

```python
import functools
import math

import jax
import jax.numpy as jnp
from jax import lax
from jax.sharding import PartitionSpec as P

HEADS = 16
HEAD_DIM = 64
ROT = 32


epsilon = 1e-05


def layer_norm(rows, gain, shift):
    center = jnp.mean(rows, axis=-1, keepdims=True)
    spread = rows - center
    variance = jnp.mean(spread * spread, axis=-1, keepdims=True)
    return spread * lax.rsqrt(variance + epsilon) * gain + shift


def rotary_tables(length):
    position = jnp.arange(length).astype(jnp.float32)[:, None]
    ladder = jnp.arange(ROT // 2).astype(jnp.float32) * (-2.0 * math.log(10000.0) / ROT)
    angle = position * jnp.exp(ladder)[None, :]
    return (jnp.cos(angle)[:, None, :], jnp.sin(angle)[:, None, :])


def rotate(field, cosine, sine):
    paired = field[..., :ROT].reshape(field.shape[:-1] + (ROT // 2, 2))
    first = paired[..., 0]
    second = paired[..., 1]
    turned = jnp.stack([first * cosine - second * sine, second * cosine + first * sine], axis=-1)
    return jnp.concatenate([turned.reshape(field.shape[:-1] + (ROT,)), field[..., ROT:]], axis=-1)


def allowed_keys(first, count, length, seq_len):
    query_place = first + jnp.arange(count)[:, None]
    key_place = jnp.arange(seq_len)[None, :]
    return (key_place <= query_place) & (key_place < length)


def attend_forward(item):
    query, keys, values, length = item
    seq_len = keys.shape[0]
    block = min(512, seq_len)
    results = []
    logsums = []
    for first in range(0, seq_len, block):
        scores = jnp.einsum(
            "qhd,khd->hqk", query[first : first + block], keys, preferred_element_type=jnp.float32
        ) * HEAD_DIM ** (-0.5)
        masked = jnp.where(allowed_keys(first, block, length, seq_len)[None], scores, -1000000000.0)
        top = jnp.max(masked, axis=-1, keepdims=True)
        weights = jnp.exp(masked - top)
        total = jnp.sum(weights, axis=-1, keepdims=True)
        probs = (weights / total).astype(jnp.bfloat16)
        results.append(
            jnp.einsum("hqk,khd->qhd", probs, values, preferred_element_type=jnp.float32)
        )
        logsums.append(top + jnp.log(total))
    return (jnp.concatenate(results, axis=0).astype(jnp.bfloat16), jnp.concatenate(logsums, axis=1))


def attend_backward(item):
    query, keys, values, upstream, logsum, length = item
    seq_len = keys.shape[0]
    block = min(512, seq_len)
    scale = HEAD_DIM ** (-0.5)
    query_parts = []
    key_grad = jnp.zeros(keys.shape, jnp.float32)
    value_grad = jnp.zeros(values.shape, jnp.float32)
    for first in range(0, seq_len, block):
        query_rows = query[first : first + block]
        upstream_rows = upstream[first : first + block]
        scores = (
            jnp.einsum("qhd,khd->hqk", query_rows, keys, preferred_element_type=jnp.float32) * scale
        )
        masked = jnp.where(allowed_keys(first, block, length, seq_len)[None], scores, -1000000000.0)
        probs = jnp.exp(masked - logsum[:, first : first + block])
        upward = jnp.einsum(
            "qhd,khd->hqk", upstream_rows, values, preferred_element_type=jnp.float32
        )
        inner = jnp.sum(probs * upward, axis=-1, keepdims=True)
        score_grad = (probs * (upward - inner)).astype(jnp.bfloat16)
        query_parts.append(
            jnp.einsum("hqk,khd->qhd", score_grad, keys, preferred_element_type=jnp.float32) * scale
        )
        key_grad = (
            key_grad
            + jnp.einsum("hqk,qhd->khd", score_grad, query_rows, preferred_element_type=jnp.float32)
            * scale
        )
        value_grad = value_grad + jnp.einsum(
            "hqk,qhd->khd",
            probs.astype(jnp.bfloat16),
            upstream_rows,
            preferred_element_type=jnp.float32,
        )
    return (jnp.concatenate(query_parts, axis=0), key_grad, value_grad)


def gelu_tanh(inner):
    return jax.nn.gelu(inner, approximate=True)


ALL = ("dp", "fsdp")


PACK = 6144


def padded(flat, axis):
    size = sum(item.shape[axis] for item in flat)
    extra = -size % PACK
    if extra:
        shape = list(flat[0].shape)
        shape[axis] = extra
        flat = flat + [jnp.zeros(shape, flat[0].dtype)]
    return jnp.concatenate(flat, axis=axis)


def gather_packed(parts):
    flat = [part.reshape(-1) for part in parts]
    packed = padded(flat, 0)
    full = lax.all_gather(packed, ALL, axis=0, tiled=False)
    pieces = []
    offset = 0
    for part, item in zip(parts, flat):
        size = item.shape[0]
        piece = full[:, offset : offset + size]
        pieces.append(piece.reshape((full.shape[0] * part.shape[0],) + part.shape[1:]))
        offset += size
    return pieces


SCATTER_ROWS = 8
SCATTER_COLUMNS = 768


def pack_for_scatter(parts, count):
    flat = [part.astype(jnp.bfloat16).reshape(count, -1) for part in parts]
    size = sum(item.shape[1] for item in flat)
    extra = -size % (SCATTER_ROWS * SCATTER_COLUMNS)
    if extra:
        flat = flat + [jnp.zeros((count, extra), jnp.bfloat16)]
    return jnp.concatenate(flat, axis=1).reshape(count * SCATTER_ROWS, -1)


def scatter_packed(packed, parts, count):
    summed = lax.psum_scatter(packed, ALL, scatter_dimension=0, tiled=True).reshape(-1)
    pieces = []
    offset = 0
    for part in parts:
        size = part.size // count
        piece = summed[offset : offset + size].astype(jnp.float32)
        pieces.append(piece.reshape((part.shape[0] // count,) + part.shape[1:]))
        offset += size
    return pieces


def body(
    tokens,
    lengths,
    attend_weight,
    project_weight,
    expand_weight,
    contract_weight,
    inner_bias,
    outer_bias,
    norm_gain,
    norm_shift,
    cotangent,
    *,
    count,
):
    seq_dev, seq_len, width = tokens.shape
    positions = seq_dev * seq_len
    attend_full, gain_full, shift_full, inner_full, outer_full = gather_packed(
        [attend_weight, norm_gain, norm_shift, inner_bias, outer_bias]
    )
    expand_full, project_full, contract_full = gather_packed(
        [expand_weight, project_weight, contract_weight]
    )
    rows = tokens.reshape(positions, width).astype(jnp.float32)
    normed, norm_pull = jax.vjp(
        layer_norm, rows, gain_full.astype(jnp.float32), shift_full.astype(jnp.float32)
    )
    normed_low = normed.astype(jnp.bfloat16)
    triple = jnp.dot(normed_low, attend_full, preferred_element_type=jnp.float32).reshape(
        seq_dev, seq_len, 3, HEADS, HEAD_DIM
    )
    cosine, sine = rotary_tables(seq_len)

    def turn(query, keys):
        return (rotate(query, cosine, sine), rotate(keys, cosine, sine))

    (query, keys), turn_pull = jax.vjp(turn, triple[:, :, 0], triple[:, :, 1])
    query_low = query.astype(jnp.bfloat16)
    keys_low = keys.astype(jnp.bfloat16)
    values_low = triple[:, :, 2].astype(jnp.bfloat16)
    attended, logsums = lax.map(attend_forward, (query_low, keys_low, values_low, lengths))
    mixed_low = attended.reshape(positions, width)
    hidden = jnp.dot(
        normed_low, expand_full, preferred_element_type=jnp.float32
    ) + inner_full.astype(jnp.float32)
    active, gelu_pull = jax.vjp(gelu_tanh, hidden)
    active_low = active.astype(jnp.bfloat16)
    result = rows + jnp.dot(mixed_low, project_full, preferred_element_type=jnp.float32)
    result = (
        result
        + jnp.dot(active_low, contract_full, preferred_element_type=jnp.float32)
        + outer_full.astype(jnp.float32)
    )
    output = result.astype(jnp.bfloat16).reshape(tokens.shape)
    upstream = cotangent.reshape(positions, width)
    outer_grad = jnp.sum(upstream, axis=0, dtype=jnp.float32)
    contract_grad = jnp.einsum(
        "tf,td->fd", active_low, upstream, preferred_element_type=jnp.float32
    )
    project_grad = jnp.einsum("te,td->ed", mixed_low, upstream, preferred_element_type=jnp.float32)
    active_grad = jnp.einsum(
        "td,fd->tf", upstream, contract_full, preferred_element_type=jnp.float32
    )
    hidden_grad = gelu_pull(active_grad)[0].astype(jnp.bfloat16)
    expand_grad = jnp.einsum(
        "te,tf->ef", normed_low, hidden_grad, preferred_element_type=jnp.float32
    )
    inner_grad = jnp.sum(hidden_grad, axis=0, dtype=jnp.float32)
    early = [contract_grad, project_grad, expand_grad, inner_grad, outer_grad]
    early_packed = pack_for_scatter(early, count)
    normed_grad = jnp.einsum(
        "tf,ef->te", hidden_grad, expand_full, preferred_element_type=jnp.float32
    )
    mixed_grad = jnp.einsum("td,ed->te", upstream, project_full, preferred_element_type=jnp.float32)
    mixed_grad = mixed_grad.astype(jnp.bfloat16).reshape(seq_dev, seq_len, HEADS, HEAD_DIM)
    early_packed, mixed_grad = lax.optimization_barrier((early_packed, mixed_grad))
    contract_part, project_part, expand_part, inner_part, outer_part = scatter_packed(
        early_packed, early, count
    )
    query_grad, key_grad, value_grad = lax.map(
        attend_backward, (query_low, keys_low, values_low, mixed_grad, logsums, lengths)
    )
    query_turned, key_turned = turn_pull((query_grad, key_grad))
    triple_grad = (
        jnp.stack([query_turned, key_turned, value_grad], axis=2)
        .reshape(positions, 3 * width)
        .astype(jnp.bfloat16)
    )
    attend_grad = jnp.einsum(
        "te,tc->ec", normed_low, triple_grad, preferred_element_type=jnp.float32
    )
    normed_grad = normed_grad + jnp.einsum(
        "tc,ec->te", triple_grad, attend_full, preferred_element_type=jnp.float32
    )
    rows_grad, gain_grad, shift_grad = norm_pull(normed_grad)
    token_grad = (
        (upstream.astype(jnp.float32) + rows_grad).astype(jnp.bfloat16).reshape(tokens.shape)
    )
    late = [attend_grad, gain_grad, shift_grad]
    attend_part, gain_part, shift_part = scatter_packed(pack_for_scatter(late, count), late, count)
    return (
        output,
        token_grad,
        attend_part,
        project_part,
        expand_part,
        contract_part,
        inner_part,
        outer_part,
        gain_part,
        shift_part,
    )


def solution(mesh):
    count = mesh.shape["dp"] * mesh.shape["fsdp"]
    return jax.shard_map(
        functools.partial(body, count=count),
        mesh=mesh,
        in_specs=(
            P(("dp", "fsdp"), None, None),
            P(("dp", "fsdp")),
            P(("dp", "fsdp"), None),
            P(("dp", "fsdp"), None),
            P(("dp", "fsdp"), None),
            P(("dp", "fsdp"), None),
            P(("dp", "fsdp")),
            P(("dp", "fsdp")),
            P(("dp", "fsdp")),
            P(("dp", "fsdp")),
            P(("dp", "fsdp"), None, None),
        ),
        out_specs=(
            P(("dp", "fsdp"), None, None),
            P(("dp", "fsdp"), None, None),
            P(("dp", "fsdp"), None),
            P(("dp", "fsdp"), None),
            P(("dp", "fsdp"), None),
            P(("dp", "fsdp"), None),
            P(("dp", "fsdp")),
            P(("dp", "fsdp")),
            P(("dp", "fsdp")),
            P(("dp", "fsdp")),
        ),
        check_vma=False,
    )
```

```python
import math

import jax
import jax.numpy as jnp
from jax import lax
from jax.sharding import PartitionSpec as P


HEADS = 16
HEAD_DIM = 64
ROT = 32


epsilon = 1e-05


def layer_norm(rows, gain, shift):
    center = jnp.mean(rows, axis=-1, keepdims=True)
    spread = rows - center
    variance = jnp.mean(spread * spread, axis=-1, keepdims=True)
    return spread * lax.rsqrt(variance + epsilon) * gain + shift


def rotary_tables(length):
    position = jnp.arange(length).astype(jnp.float32)[:, None]
    ladder = jnp.arange(ROT // 2).astype(jnp.float32) * (-2.0 * math.log(10000.0) / ROT)
    angle = position * jnp.exp(ladder)[None, :]
    return (jnp.cos(angle)[:, None, :], jnp.sin(angle)[:, None, :])


def rotate(field, cosine, sine):
    paired = field[..., :ROT].reshape(field.shape[:-1] + (ROT // 2, 2))
    first = paired[..., 0]
    second = paired[..., 1]
    turned = jnp.stack([first * cosine - second * sine, second * cosine + first * sine], axis=-1)
    return jnp.concatenate([turned.reshape(field.shape[:-1] + (ROT,)), field[..., ROT:]], axis=-1)


def allowed_keys(first, count, length, seq_len):
    query_place = first + jnp.arange(count)[:, None]
    key_place = jnp.arange(seq_len)[None, :]
    return (key_place <= query_place) & (key_place < length)


def attend_forward(item):
    query, keys, values, length = item
    seq_len = keys.shape[0]
    block = min(512, seq_len)
    results = []
    logsums = []
    for first in range(0, seq_len, block):
        scores = jnp.einsum(
            "qhd,khd->hqk", query[first : first + block], keys, preferred_element_type=jnp.float32
        ) * HEAD_DIM ** (-0.5)
        masked = jnp.where(allowed_keys(first, block, length, seq_len)[None], scores, -1000000000.0)
        top = jnp.max(masked, axis=-1, keepdims=True)
        weights = jnp.exp(masked - top)
        total = jnp.sum(weights, axis=-1, keepdims=True)
        probs = (weights / total).astype(jnp.bfloat16)
        results.append(
            jnp.einsum("hqk,khd->qhd", probs, values, preferred_element_type=jnp.float32)
        )
        logsums.append(top + jnp.log(total))
    return (jnp.concatenate(results, axis=0).astype(jnp.bfloat16), jnp.concatenate(logsums, axis=1))


def attend_backward(item):
    query, keys, values, upstream, logsum, length = item
    seq_len = keys.shape[0]
    block = min(512, seq_len)
    scale = HEAD_DIM ** (-0.5)
    query_parts = []
    key_grad = jnp.zeros(keys.shape, jnp.float32)
    value_grad = jnp.zeros(values.shape, jnp.float32)
    for first in range(0, seq_len, block):
        query_rows = query[first : first + block]
        upstream_rows = upstream[first : first + block]
        scores = (
            jnp.einsum("qhd,khd->hqk", query_rows, keys, preferred_element_type=jnp.float32) * scale
        )
        masked = jnp.where(allowed_keys(first, block, length, seq_len)[None], scores, -1000000000.0)
        probs = jnp.exp(masked - logsum[:, first : first + block])
        upward = jnp.einsum(
            "qhd,khd->hqk", upstream_rows, values, preferred_element_type=jnp.float32
        )
        inner = jnp.sum(probs * upward, axis=-1, keepdims=True)
        score_grad = (probs * (upward - inner)).astype(jnp.bfloat16)
        query_parts.append(
            jnp.einsum("hqk,khd->qhd", score_grad, keys, preferred_element_type=jnp.float32) * scale
        )
        key_grad = (
            key_grad
            + jnp.einsum("hqk,qhd->khd", score_grad, query_rows, preferred_element_type=jnp.float32)
            * scale
        )
        value_grad = value_grad + jnp.einsum(
            "hqk,qhd->khd",
            probs.astype(jnp.bfloat16),
            upstream_rows,
            preferred_element_type=jnp.float32,
        )
    return (jnp.concatenate(query_parts, axis=0), key_grad, value_grad)


def gelu_tanh(inner):
    return jax.nn.gelu(inner, approximate=True)


ALL = ("dp", "fsdp")


PACK = 6144


def padded(flat, axis):
    size = sum(item.shape[axis] for item in flat)
    extra = -size % PACK
    if extra:
        shape = list(flat[0].shape)
        shape[axis] = extra
        flat = flat + [jnp.zeros(shape, flat[0].dtype)]
    return jnp.concatenate(flat, axis=axis)


def gather_packed(parts):
    flat = [part.reshape(-1) for part in parts]
    packed = padded(flat, 0)
    full = lax.all_gather(packed, ALL, axis=0, tiled=False)
    pieces = []
    offset = 0
    for part, item in zip(parts, flat):
        size = item.shape[0]
        piece = full[:, offset : offset + size]
        pieces.append(piece.reshape((full.shape[0] * part.shape[0],) + part.shape[1:]))
        offset += size
    return pieces


SCATTER_ROWS = 8
SCATTER_COLUMNS = 768


def pack_for_scatter(parts, count):
    flat = [part.astype(jnp.bfloat16).reshape(count, -1) for part in parts]
    size = sum(item.shape[1] for item in flat)
    extra = -size % (SCATTER_ROWS * SCATTER_COLUMNS)
    if extra:
        flat = flat + [jnp.zeros((count, extra), jnp.bfloat16)]
    return jnp.concatenate(flat, axis=1).reshape(count * SCATTER_ROWS, -1)


def scatter_packed(packed, parts, count):
    summed = lax.psum_scatter(packed, ALL, scatter_dimension=0, tiled=True)
    summed = summed.reshape(-1)
    pieces = []
    offset = 0
    for part in parts:
        size = part.size // count
        piece = summed[offset : offset + size].astype(jnp.float32)
        pieces.append(piece.reshape((part.shape[0] // count,) + part.shape[1:]))
        offset += size
    return pieces


def body(
    tokens,
    lengths,
    attend_weight,
    project_weight,
    expand_weight,
    contract_weight,
    inner_bias,
    outer_bias,
    norm_gain,
    norm_shift,
    cotangent,
    *,
    count,
):
    seq_dev, seq_len, width = tokens.shape
    positions = seq_dev * seq_len
    attend_full, gain_full, shift_full, inner_full, outer_full = gather_packed(
        [attend_weight, norm_gain, norm_shift, inner_bias, outer_bias]
    )
    expand_full, project_full, contract_full = gather_packed(
        [expand_weight, project_weight, contract_weight]
    )
    rows = tokens.reshape(positions, width).astype(jnp.float32)
    normed, norm_pull = jax.vjp(
        layer_norm, rows, gain_full.astype(jnp.float32), shift_full.astype(jnp.float32)
    )
    normed_low = normed.astype(jnp.bfloat16)
    triple = jnp.dot(normed_low, attend_full, preferred_element_type=jnp.float32).reshape(
        seq_dev, seq_len, 3, HEADS, HEAD_DIM
    )
    cosine, sine = rotary_tables(seq_len)

    def turn(query, keys):
        return (rotate(query, cosine, sine), rotate(keys, cosine, sine))

    (query, keys), turn_pull = jax.vjp(turn, triple[:, :, 0], triple[:, :, 1])
    query_low = query.astype(jnp.bfloat16)
    keys_low = keys.astype(jnp.bfloat16)
    values_low = triple[:, :, 2].astype(jnp.bfloat16)
    attended, logsums = lax.map(attend_forward, (query_low, keys_low, values_low, lengths))
    mixed_low = attended.reshape(positions, width)
    hidden = jnp.dot(
        normed_low, expand_full, preferred_element_type=jnp.float32
    ) + inner_full.astype(jnp.float32)
    active, gelu_pull = jax.vjp(gelu_tanh, hidden)
    active_low = active.astype(jnp.bfloat16)
    result = rows + jnp.dot(mixed_low, project_full, preferred_element_type=jnp.float32)
    result = (
        result
        + jnp.dot(active_low, contract_full, preferred_element_type=jnp.float32)
        + outer_full.astype(jnp.float32)
    )
    output = result.astype(jnp.bfloat16).reshape(tokens.shape)
    upstream = cotangent.reshape(positions, width)
    outer_grad = jnp.sum(upstream, axis=0, dtype=jnp.float32)
    contract_grad = jnp.einsum(
        "tf,td->fd", active_low, upstream, preferred_element_type=jnp.float32
    )
    project_grad = jnp.einsum("te,td->ed", mixed_low, upstream, preferred_element_type=jnp.float32)
    active_grad = jnp.einsum(
        "td,fd->tf", upstream, contract_full, preferred_element_type=jnp.float32
    )
    hidden_grad = gelu_pull(active_grad)[0].astype(jnp.bfloat16)
    expand_grad = jnp.einsum(
        "te,tf->ef", normed_low, hidden_grad, preferred_element_type=jnp.float32
    )
    inner_grad = jnp.sum(hidden_grad, axis=0, dtype=jnp.float32)
    early = [contract_grad, project_grad, expand_grad, inner_grad, outer_grad]
    early_packed = pack_for_scatter(early, count)
    normed_grad = jnp.einsum(
        "tf,ef->te", hidden_grad, expand_full, preferred_element_type=jnp.float32
    )
    mixed_grad = jnp.einsum("td,ed->te", upstream, project_full, preferred_element_type=jnp.float32)
    mixed_grad = mixed_grad.astype(jnp.bfloat16).reshape(seq_dev, seq_len, HEADS, HEAD_DIM)
    early_packed, mixed_grad = lax.optimization_barrier((early_packed, mixed_grad))
    contract_part, project_part, expand_part, inner_part, outer_part = scatter_packed(
        early_packed, early, count
    )
    query_grad, key_grad, value_grad = lax.map(
        attend_backward, (query_low, keys_low, values_low, mixed_grad, logsums, lengths)
    )
    query_turned, key_turned = turn_pull((query_grad, key_grad))
    triple_grad = (
        jnp.stack([query_turned, key_turned, value_grad], axis=2)
        .reshape(positions, 3 * width)
        .astype(jnp.bfloat16)
    )
    attend_grad = jnp.einsum(
        "te,tc->ec", normed_low, triple_grad, preferred_element_type=jnp.float32
    )
    normed_grad = normed_grad + jnp.einsum(
        "tc,ec->te", triple_grad, attend_full, preferred_element_type=jnp.float32
    )
    rows_grad, gain_grad, shift_grad = norm_pull(normed_grad)
    token_grad = (
        (upstream.astype(jnp.float32) + rows_grad).astype(jnp.bfloat16).reshape(tokens.shape)
    )
    late = [attend_grad, gain_grad, shift_grad]
    attend_part, gain_part, shift_part = scatter_packed(pack_for_scatter(late, count), late, count)
    return (
        output,
        token_grad,
        attend_part,
        project_part,
        expand_part,
        contract_part,
        inner_part,
        outer_part,
        gain_part,
        shift_part,
    )


def solution(mesh):
    count = mesh.shape["dp"] * mesh.shape["fsdp"]

    def layer_body(*args):
        return body(*args, count=count)

    return jax.shard_map(
        layer_body,
        mesh=mesh,
        in_specs=(
            P(("dp", "fsdp"), None, None),
            P(("dp", "fsdp")),
            P(("dp", "fsdp"), None),
            P(("dp", "fsdp"), None),
            P(("dp", "fsdp"), None),
            P(("dp", "fsdp"), None),
            P(("dp", "fsdp")),
            P(("dp", "fsdp")),
            P(("dp", "fsdp")),
            P(("dp", "fsdp")),
            P(("dp", "fsdp"), None, None),
        ),
        out_specs=(
            P(("dp", "fsdp"), None, None),
            P(("dp", "fsdp"), None, None),
            P(("dp", "fsdp"), None),
            P(("dp", "fsdp"), None),
            P(("dp", "fsdp"), None),
            P(("dp", "fsdp"), None),
            P(("dp", "fsdp")),
            P(("dp", "fsdp")),
            P(("dp", "fsdp")),
            P(("dp", "fsdp")),
        ),
        check_vma=False,
    )
```

```python
import math

import jax
import jax.numpy as jnp
from jax import lax
from jax.sharding import PartitionSpec as P


HEADS = 16
HEAD_DIM = 64
ROT = 32


epsilon = 1e-05


def layer_norm(rows, gain, shift):
    center = jnp.mean(rows, axis=-1, keepdims=True)
    spread = rows - center
    variance = jnp.mean(spread * spread, axis=-1, keepdims=True)
    return spread * lax.rsqrt(variance + epsilon) * gain + shift


def rotary_tables(length):
    position = jnp.arange(length).astype(jnp.float32)[:, None]
    ladder = jnp.arange(ROT // 2).astype(jnp.float32) * (-2.0 * math.log(10000.0) / ROT)
    angle = position * jnp.exp(ladder)[None, :]
    return (jnp.cos(angle)[:, None, :], jnp.sin(angle)[:, None, :])


def rotate(field, cosine, sine):
    paired = field[..., :ROT].reshape(field.shape[:-1] + (ROT // 2, 2))
    first = paired[..., 0]
    second = paired[..., 1]
    turned = jnp.stack([first * cosine - second * sine, second * cosine + first * sine], axis=-1)
    return jnp.concatenate([turned.reshape(field.shape[:-1] + (ROT,)), field[..., ROT:]], axis=-1)


def allowed_keys(first, count, length, seq_len):
    query_place = first + jnp.arange(count)[:, None]
    key_place = jnp.arange(seq_len)[None, :]
    return (key_place <= query_place) & (key_place < length)


def attend_forward(item):
    query, keys, values, length = item
    seq_len = keys.shape[0]
    block = min(512, seq_len)
    results = []
    logsums = []
    for first in range(0, seq_len, block):
        scores = jnp.einsum(
            "qhd,khd->hqk", query[first : first + block], keys, preferred_element_type=jnp.float32
        ) * HEAD_DIM ** (-0.5)
        masked = jnp.where(allowed_keys(first, block, length, seq_len)[None], scores, -1000000000.0)
        top = jnp.max(masked, axis=-1, keepdims=True)
        weights = jnp.exp(masked - top)
        total = jnp.sum(weights, axis=-1, keepdims=True)
        probs = (weights / total).astype(jnp.bfloat16)
        results.append(
            jnp.einsum("hqk,khd->qhd", probs, values, preferred_element_type=jnp.float32)
        )
        logsums.append(top + jnp.log(total))
    return (jnp.concatenate(results, axis=0).astype(jnp.bfloat16), jnp.concatenate(logsums, axis=1))


def attend_backward(item):
    query, keys, values, upstream, logsum, length = item
    seq_len = keys.shape[0]
    block = min(512, seq_len)
    scale = HEAD_DIM ** (-0.5)
    query_parts = []
    key_grad = jnp.zeros(keys.shape, jnp.float32)
    value_grad = jnp.zeros(values.shape, jnp.float32)
    for first in range(0, seq_len, block):
        query_rows = query[first : first + block]
        upstream_rows = upstream[first : first + block]
        scores = (
            jnp.einsum("qhd,khd->hqk", query_rows, keys, preferred_element_type=jnp.float32) * scale
        )
        masked = jnp.where(allowed_keys(first, block, length, seq_len)[None], scores, -1000000000.0)
        probs = jnp.exp(masked - logsum[:, first : first + block])
        upward = jnp.einsum(
            "qhd,khd->hqk", upstream_rows, values, preferred_element_type=jnp.float32
        )
        inner = jnp.sum(probs * upward, axis=-1, keepdims=True)
        score_grad = (probs * (upward - inner)).astype(jnp.bfloat16)
        query_parts.append(
            jnp.einsum("hqk,khd->qhd", score_grad, keys, preferred_element_type=jnp.float32) * scale
        )
        key_grad = (
            key_grad
            + jnp.einsum("hqk,qhd->khd", score_grad, query_rows, preferred_element_type=jnp.float32)
            * scale
        )
        value_grad = value_grad + jnp.einsum(
            "hqk,qhd->khd",
            probs.astype(jnp.bfloat16),
            upstream_rows,
            preferred_element_type=jnp.float32,
        )
    return (jnp.concatenate(query_parts, axis=0), key_grad, value_grad)


def gelu_tanh(inner):
    return jax.nn.gelu(inner, approximate=True)


ALL = ("dp", "fsdp")


COLUMNS = 384


def pad_columns(blocks):
    width = sum(block.shape[1] for block in blocks)
    extra = -width % COLUMNS
    if extra:
        blocks = blocks + [jnp.zeros((blocks[0].shape[0], extra), blocks[0].dtype)]
    return jnp.concatenate(blocks, axis=1)


def split_columns(packed, widths):
    pieces = []
    offset = 0
    for width in widths:
        pieces.append(packed[:, offset : offset + width])
        offset += width
    return pieces


def gather_columns(blocks):
    packed = pad_columns(blocks)
    full = lax.all_gather(packed[None], ALL, axis=0, tiled=True)
    full = full.reshape(full.shape[0] * full.shape[1], full.shape[2])
    return split_columns(full, [block.shape[1] for block in blocks])


def scatter_columns(packed, widths):
    summed = lax.psum_scatter(packed, ALL, scatter_dimension=0, tiled=True)
    return [piece.astype(jnp.float32) for piece in split_columns(summed, widths)]


def as_column(vector, rows):
    return vector.reshape(rows, -1)


def body(
    tokens,
    lengths,
    attend_weight,
    project_weight,
    expand_weight,
    contract_weight,
    inner_bias,
    outer_bias,
    norm_gain,
    norm_shift,
    cotangent,
):
    seq_dev, seq_len, width = tokens.shape
    positions = seq_dev * seq_len
    rows_dev = attend_weight.shape[0]
    attend_full, gain_full, shift_full, inner_full, outer_full = gather_columns(
        [
            attend_weight,
            as_column(norm_gain, rows_dev),
            as_column(norm_shift, rows_dev),
            as_column(inner_bias, rows_dev),
            as_column(outer_bias, rows_dev),
        ]
    )
    gain_full = gain_full.reshape(-1)
    shift_full = shift_full.reshape(-1)
    inner_full = inner_full.reshape(-1)
    outer_full = outer_full.reshape(-1)
    expand_full, project_full, contract_full = gather_columns(
        [expand_weight, project_weight, contract_weight.reshape(rows_dev, -1)]
    )
    contract_full = contract_full.reshape(-1, width)
    rows = tokens.reshape(positions, width).astype(jnp.float32)
    normed, norm_pull = jax.vjp(
        layer_norm, rows, gain_full.astype(jnp.float32), shift_full.astype(jnp.float32)
    )
    normed_low = normed.astype(jnp.bfloat16)
    triple = jnp.dot(normed_low, attend_full, preferred_element_type=jnp.float32).reshape(
        seq_dev, seq_len, 3, HEADS, HEAD_DIM
    )
    cosine, sine = rotary_tables(seq_len)

    def turn(query, keys):
        return (rotate(query, cosine, sine), rotate(keys, cosine, sine))

    (query, keys), turn_pull = jax.vjp(turn, triple[:, :, 0], triple[:, :, 1])
    query_low = query.astype(jnp.bfloat16)
    keys_low = keys.astype(jnp.bfloat16)
    values_low = triple[:, :, 2].astype(jnp.bfloat16)
    attended, logsums = lax.map(attend_forward, (query_low, keys_low, values_low, lengths))
    mixed_low = attended.reshape(positions, width)
    hidden = jnp.dot(
        normed_low, expand_full, preferred_element_type=jnp.float32
    ) + inner_full.astype(jnp.float32)
    active, gelu_pull = jax.vjp(gelu_tanh, hidden)
    active_low = active.astype(jnp.bfloat16)
    result = rows + jnp.dot(mixed_low, project_full, preferred_element_type=jnp.float32)
    result = (
        result
        + jnp.dot(active_low, contract_full, preferred_element_type=jnp.float32)
        + outer_full.astype(jnp.float32)
    )
    output = result.astype(jnp.bfloat16).reshape(tokens.shape)
    upstream = cotangent.reshape(positions, width)
    outer_grad = jnp.sum(upstream, axis=0, dtype=jnp.float32)
    contract_grad = jnp.einsum(
        "tf,td->fd", active_low, upstream, preferred_element_type=jnp.float32
    )
    project_grad = jnp.einsum("te,td->ed", mixed_low, upstream, preferred_element_type=jnp.float32)
    active_grad = jnp.einsum(
        "td,fd->tf", upstream, contract_full, preferred_element_type=jnp.float32
    )
    hidden_grad = gelu_pull(active_grad)[0].astype(jnp.bfloat16)
    expand_grad = jnp.einsum(
        "te,tf->ef", normed_low, hidden_grad, preferred_element_type=jnp.float32
    )
    inner_grad = jnp.sum(hidden_grad, axis=0, dtype=jnp.float32)
    rows_all = expand_grad.shape[0]
    early = [
        expand_grad.astype(jnp.bfloat16),
        contract_grad.astype(jnp.bfloat16).reshape(rows_all, -1),
        project_grad.astype(jnp.bfloat16),
        as_column(inner_grad.astype(jnp.bfloat16), rows_all),
        as_column(outer_grad.astype(jnp.bfloat16), rows_all),
    ]
    early_widths = [block.shape[1] for block in early]
    early_packed = pad_columns(early)
    normed_grad = jnp.einsum(
        "tf,ef->te", hidden_grad, expand_full, preferred_element_type=jnp.float32
    )
    mixed_grad = jnp.einsum("td,ed->te", upstream, project_full, preferred_element_type=jnp.float32)
    mixed_grad = mixed_grad.astype(jnp.bfloat16).reshape(seq_dev, seq_len, HEADS, HEAD_DIM)
    early_packed, mixed_grad = lax.optimization_barrier((early_packed, mixed_grad))
    expand_part, contract_part, project_part, inner_part, outer_part = scatter_columns(
        early_packed, early_widths
    )
    contract_part = contract_part.reshape(-1, width)
    inner_part = inner_part.reshape(-1)
    outer_part = outer_part.reshape(-1)
    query_grad, key_grad, value_grad = lax.map(
        attend_backward, (query_low, keys_low, values_low, mixed_grad, logsums, lengths)
    )
    query_turned, key_turned = turn_pull((query_grad, key_grad))
    triple_grad = (
        jnp.stack([query_turned, key_turned, value_grad], axis=2)
        .reshape(positions, 3 * width)
        .astype(jnp.bfloat16)
    )
    attend_grad = jnp.einsum(
        "te,tc->ec", normed_low, triple_grad, preferred_element_type=jnp.float32
    )
    normed_grad = normed_grad + jnp.einsum(
        "tc,ec->te", triple_grad, attend_full, preferred_element_type=jnp.float32
    )
    rows_grad, gain_grad, shift_grad = norm_pull(normed_grad)
    token_grad = (
        (upstream.astype(jnp.float32) + rows_grad).astype(jnp.bfloat16).reshape(tokens.shape)
    )
    late = [
        attend_grad.astype(jnp.bfloat16),
        as_column(gain_grad.astype(jnp.bfloat16), rows_all),
        as_column(shift_grad.astype(jnp.bfloat16), rows_all),
    ]
    attend_part, gain_part, shift_part = scatter_columns(
        pad_columns(late), [block.shape[1] for block in late]
    )
    gain_part = gain_part.reshape(-1)
    shift_part = shift_part.reshape(-1)
    return (
        output,
        token_grad,
        attend_part,
        project_part,
        expand_part,
        contract_part,
        inner_part,
        outer_part,
        gain_part,
        shift_part,
    )


def solution(mesh):
    return jax.shard_map(
        body,
        mesh=mesh,
        in_specs=(
            P(("dp", "fsdp"), None, None),
            P(("dp", "fsdp")),
            P(("dp", "fsdp"), None),
            P(("dp", "fsdp"), None),
            P(("dp", "fsdp"), None),
            P(("dp", "fsdp"), None),
            P(("dp", "fsdp")),
            P(("dp", "fsdp")),
            P(("dp", "fsdp")),
            P(("dp", "fsdp")),
            P(("dp", "fsdp"), None, None),
        ),
        out_specs=(
            P(("dp", "fsdp"), None, None),
            P(("dp", "fsdp"), None, None),
            P(("dp", "fsdp"), None),
            P(("dp", "fsdp"), None),
            P(("dp", "fsdp"), None),
            P(("dp", "fsdp"), None),
            P(("dp", "fsdp")),
            P(("dp", "fsdp")),
            P(("dp", "fsdp")),
            P(("dp", "fsdp")),
        ),
        check_vma=False,
    )
```

```python
import math

import jax
import jax.numpy as jnp
from jax import lax
from jax.experimental import pallas as pl
from jax.experimental.pallas import tpu as pltpu
from jax.sharding import PartitionSpec as P


HEADS = 16
HEAD_DIM = 64
ROT = 32


epsilon = 1e-05


def layer_norm(rows, gain, shift):
    center = jnp.mean(rows, axis=-1, keepdims=True)
    spread = rows - center
    variance = jnp.mean(spread * spread, axis=-1, keepdims=True)
    return spread * lax.rsqrt(variance + epsilon) * gain + shift


def rotary_tables(length):
    position = jnp.arange(length).astype(jnp.float32)[:, None]
    ladder = jnp.arange(ROT // 2).astype(jnp.float32) * (-2.0 * math.log(10000.0) / ROT)
    angle = position * jnp.exp(ladder)[None, :]
    return (jnp.cos(angle)[:, None, :], jnp.sin(angle)[:, None, :])


def rotate(field, cosine, sine):
    paired = field[..., :ROT].reshape(field.shape[:-1] + (ROT // 2, 2))
    first = paired[..., 0]
    second = paired[..., 1]
    turned = jnp.stack([first * cosine - second * sine, second * cosine + first * sine], axis=-1)
    return jnp.concatenate([turned.reshape(field.shape[:-1] + (ROT,)), field[..., ROT:]], axis=-1)


QUERY_BLOCK = 256
NT = (((1,), (1,)), ((), ()))
TN = (((0,), (0,)), ((), ()))


def head_scores(q, k, first, length, lane_mask):
    scores = lax.dot_general(
        jnp.where(lane_mask, q, jnp.zeros_like(q)), k, NT, preferred_element_type=jnp.float32
    ) * HEAD_DIM ** (-0.5)
    query_place = first + lax.broadcasted_iota(jnp.int32, scores.shape, 0)
    key_place = lax.broadcasted_iota(jnp.int32, scores.shape, 1)
    allowed = (key_place <= query_place) & (key_place < length)
    return jnp.where(allowed, scores, -1000000000.0)


def attention_forward_kernel(length_ref, q_ref, k_ref, v_ref, o_ref, top_ref, total_ref):
    block = q_ref.shape[0]
    first = pl.program_id(1) * block
    length = length_ref[0]
    q = q_ref[...]
    k = k_ref[...]
    v = v_ref[...]
    lanes = lax.broadcasted_iota(jnp.int32, q.shape, 1)
    result = None
    for head in range(2):
        lane_mask = (lanes >= head * HEAD_DIM) & (lanes < (head + 1) * HEAD_DIM)
        masked = head_scores(q, k, first, length, lane_mask)
        top = jnp.max(masked, axis=-1, keepdims=True)
        weights = jnp.exp(masked - top)
        total = jnp.sum(weights, axis=-1, keepdims=True)
        probs = (weights / total).astype(jnp.bfloat16)
        out = jnp.dot(probs, v, preferred_element_type=jnp.float32)
        result = out if result is None else jnp.where(lane_mask, out, result)
        top_ref[head] = top
        total_ref[head] = total
    o_ref[...] = result.astype(o_ref.dtype)


def attention_backward_kernel(
    length_ref, q_ref, k_ref, v_ref, g_ref, top_ref, total_ref, dq_ref, dk_ref, dv_ref
):
    block = q_ref.shape[0]
    step = pl.program_id(1)
    first = step * block
    length = length_ref[0]
    scale = HEAD_DIM ** (-0.5)

    @pl.when(step == 0)
    def _():
        dk_ref[...] = jnp.zeros_like(dk_ref)
        dv_ref[...] = jnp.zeros_like(dv_ref)

    q = q_ref[...]
    k = k_ref[...]
    v = v_ref[...]
    g = g_ref[...]
    lanes = lax.broadcasted_iota(jnp.int32, q.shape, 1)
    key_lanes = lax.broadcasted_iota(jnp.int32, k.shape, 1)
    dq = None
    dk = None
    dv = None
    for head in range(2):
        lane_mask = (lanes >= head * HEAD_DIM) & (lanes < (head + 1) * HEAD_DIM)
        key_mask = (key_lanes >= head * HEAD_DIM) & (key_lanes < (head + 1) * HEAD_DIM)
        masked = head_scores(q, k, first, length, lane_mask)
        probs = jnp.exp(masked - top_ref[head]) / total_ref[head]
        upward = lax.dot_general(
            jnp.where(lane_mask, g, jnp.zeros_like(g)), v, NT, preferred_element_type=jnp.float32
        )
        inner = jnp.sum(probs * upward, axis=-1, keepdims=True)
        score_grad = (probs * (upward - inner)).astype(jnp.bfloat16)
        dq_head = jnp.dot(score_grad, k, preferred_element_type=jnp.float32) * scale
        dk_head = lax.dot_general(score_grad, q, TN, preferred_element_type=jnp.float32) * scale
        dv_head = lax.dot_general(
            probs.astype(jnp.bfloat16), g, TN, preferred_element_type=jnp.float32
        )
        if dq is None:
            dq, dk, dv = dq_head, dk_head, dv_head
        else:
            dq = jnp.where(lane_mask, dq_head, dq)
            dk = jnp.where(key_mask, dk_head, dk)
            dv = jnp.where(key_mask, dv_head, dv)
    dq_ref[...] = dq
    dk_ref[...] += dk
    dv_ref[...] += dv


def attention_forward(q, k, v, length):
    seq, width = q.shape
    pairs = width // (2 * HEAD_DIM)
    block = min(QUERY_BLOCK, seq)
    grid = (pairs, seq // block)
    lane = 2 * HEAD_DIM
    return pl.pallas_call(
        attention_forward_kernel,
        out_shape=(
            jax.ShapeDtypeStruct((seq, width), jnp.bfloat16),
            jax.ShapeDtypeStruct((2 * pairs, seq, 1), jnp.float32),
            jax.ShapeDtypeStruct((2 * pairs, seq, 1), jnp.float32),
        ),
        grid_spec=pltpu.PrefetchScalarGridSpec(
            num_scalar_prefetch=1,
            grid=grid,
            in_specs=[
                pl.BlockSpec((block, lane), lambda p, i, n: (i, p)),
                pl.BlockSpec((seq, lane), lambda p, i, n: (0, p)),
                pl.BlockSpec((seq, lane), lambda p, i, n: (0, p)),
            ],
            out_specs=[
                pl.BlockSpec((block, lane), lambda p, i, n: (i, p)),
                pl.BlockSpec((2, block, 1), lambda p, i, n: (p, i, 0)),
                pl.BlockSpec((2, block, 1), lambda p, i, n: (p, i, 0)),
            ],
        ),
        compiler_params=pltpu.CompilerParams(dimension_semantics=("parallel", "arbitrary")),
        cost_estimate=pl.CostEstimate(
            flops=8 * seq * seq * width, transcendentals=seq * seq * pairs * 2,
            bytes_accessed=2 * seq * width * 2 * (1 + 2 * seq // block),
        ),
    )(length, q, k, v)


def attention_backward(q, k, v, g, top, total, length):
    seq, width = q.shape
    pairs = width // (2 * HEAD_DIM)
    block = min(QUERY_BLOCK, seq)
    grid = (pairs, seq // block)
    lane = 2 * HEAD_DIM
    return pl.pallas_call(
        attention_backward_kernel,
        out_shape=(
            jax.ShapeDtypeStruct((seq, width), jnp.float32),
            jax.ShapeDtypeStruct((seq, width), jnp.float32),
            jax.ShapeDtypeStruct((seq, width), jnp.float32),
        ),
        grid_spec=pltpu.PrefetchScalarGridSpec(
            num_scalar_prefetch=1,
            grid=grid,
            in_specs=[
                pl.BlockSpec((block, lane), lambda p, i, n: (i, p)),
                pl.BlockSpec((seq, lane), lambda p, i, n: (0, p)),
                pl.BlockSpec((seq, lane), lambda p, i, n: (0, p)),
                pl.BlockSpec((block, lane), lambda p, i, n: (i, p)),
                pl.BlockSpec((2, block, 1), lambda p, i, n: (p, i, 0)),
                pl.BlockSpec((2, block, 1), lambda p, i, n: (p, i, 0)),
            ],
            out_specs=[
                pl.BlockSpec((block, lane), lambda p, i, n: (i, p)),
                pl.BlockSpec((seq, lane), lambda p, i, n: (0, p)),
                pl.BlockSpec((seq, lane), lambda p, i, n: (0, p)),
            ],
        ),
        compiler_params=pltpu.CompilerParams(dimension_semantics=("parallel", "arbitrary")),
        cost_estimate=pl.CostEstimate(
            flops=20 * seq * seq * width, transcendentals=seq * seq * pairs * 2,
            bytes_accessed=2 * seq * width * 2 * (2 + 2 * seq // block) + 3 * seq * width * 4,
        ),
    )(length, q, k, v, g, top, total)


def gelu_tanh(inner):
    return jax.nn.gelu(inner, approximate=True)


ALL = ("dp", "fsdp")


COLUMNS = 384


def pad_columns(blocks):
    width = sum(block.shape[1] for block in blocks)
    extra = -width % COLUMNS
    if extra:
        blocks = blocks + [jnp.zeros((blocks[0].shape[0], extra), blocks[0].dtype)]
    return jnp.concatenate(blocks, axis=1)


def split_columns(packed, widths):
    pieces = []
    offset = 0
    for width in widths:
        pieces.append(packed[:, offset : offset + width])
        offset += width
    return pieces


def gather_columns(blocks):
    packed = pad_columns(blocks)
    full = lax.all_gather(packed[None], ALL, axis=0, tiled=True)
    full = full.reshape(full.shape[0] * full.shape[1], full.shape[2])
    return split_columns(full, [block.shape[1] for block in blocks])


def scatter_columns(packed, widths):
    summed = lax.psum_scatter(packed, ALL, scatter_dimension=0, tiled=True)
    return [piece.astype(jnp.float32) for piece in split_columns(summed, widths)]


def as_column(vector, rows):
    return vector.reshape(rows, -1)


def body(
    tokens,
    lengths,
    attend_weight,
    project_weight,
    expand_weight,
    contract_weight,
    inner_bias,
    outer_bias,
    norm_gain,
    norm_shift,
    cotangent,
):
    seq_dev, seq_len, width = tokens.shape
    positions = seq_dev * seq_len
    rows_dev = attend_weight.shape[0]
    attend_full, gain_full, shift_full, inner_full, outer_full = gather_columns(
        [
            attend_weight,
            as_column(norm_gain, rows_dev),
            as_column(norm_shift, rows_dev),
            as_column(inner_bias, rows_dev),
            as_column(outer_bias, rows_dev),
        ]
    )
    gain_full = gain_full.reshape(-1)
    shift_full = shift_full.reshape(-1)
    inner_full = inner_full.reshape(-1)
    outer_full = outer_full.reshape(-1)
    expand_full, project_full, contract_full = gather_columns(
        [expand_weight, project_weight, contract_weight.reshape(rows_dev, -1)]
    )
    contract_full = contract_full.reshape(-1, width)
    rows = tokens.reshape(positions, width).astype(jnp.float32)
    normed, norm_pull = jax.vjp(
        layer_norm, rows, gain_full.astype(jnp.float32), shift_full.astype(jnp.float32)
    )
    normed_low = normed.astype(jnp.bfloat16)
    triple = jnp.dot(normed_low, attend_full, preferred_element_type=jnp.float32).reshape(
        seq_dev, seq_len, 3, HEADS, HEAD_DIM
    )
    cosine, sine = rotary_tables(seq_len)

    def turn(query, keys):
        return (rotate(query, cosine, sine), rotate(keys, cosine, sine))

    (query, keys), turn_pull = jax.vjp(turn, triple[:, :, 0], triple[:, :, 1])
    query_low = query.astype(jnp.bfloat16)
    keys_low = keys.astype(jnp.bfloat16)
    values_low = triple[:, :, 2].astype(jnp.bfloat16)
    flat_query = query_low.reshape(seq_dev, seq_len, width)
    flat_keys = keys_low.reshape(seq_dev, seq_len, width)
    flat_values = values_low.reshape(seq_dev, seq_len, width)
    forward_parts = [
        attention_forward(flat_query[s], flat_keys[s], flat_values[s], lengths[s : s + 1])
        for s in range(seq_dev)
    ]
    mixed_low = jnp.concatenate([part[0] for part in forward_parts], axis=0)
    hidden = jnp.dot(
        normed_low, expand_full, preferred_element_type=jnp.float32
    ) + inner_full.astype(jnp.float32)
    active, gelu_pull = jax.vjp(gelu_tanh, hidden)
    active_low = active.astype(jnp.bfloat16)
    result = rows + jnp.dot(mixed_low, project_full, preferred_element_type=jnp.float32)
    result = (
        result
        + jnp.dot(active_low, contract_full, preferred_element_type=jnp.float32)
        + outer_full.astype(jnp.float32)
    )
    output = result.astype(jnp.bfloat16).reshape(tokens.shape)
    upstream = cotangent.reshape(positions, width)
    outer_grad = jnp.sum(upstream, axis=0, dtype=jnp.float32)
    contract_grad = jnp.einsum(
        "tf,td->fd", active_low, upstream, preferred_element_type=jnp.float32
    )
    project_grad = jnp.einsum("te,td->ed", mixed_low, upstream, preferred_element_type=jnp.float32)
    active_grad = jnp.einsum(
        "td,fd->tf", upstream, contract_full, preferred_element_type=jnp.float32
    )
    hidden_grad = gelu_pull(active_grad)[0].astype(jnp.bfloat16)
    expand_grad = jnp.einsum(
        "te,tf->ef", normed_low, hidden_grad, preferred_element_type=jnp.float32
    )
    inner_grad = jnp.sum(hidden_grad, axis=0, dtype=jnp.float32)
    rows_all = expand_grad.shape[0]
    early = [
        expand_grad.astype(jnp.bfloat16),
        contract_grad.astype(jnp.bfloat16).reshape(rows_all, -1),
        project_grad.astype(jnp.bfloat16),
        as_column(inner_grad.astype(jnp.bfloat16), rows_all),
        as_column(outer_grad.astype(jnp.bfloat16), rows_all),
    ]
    early_widths = [block.shape[1] for block in early]
    early_packed = pad_columns(early)
    normed_grad = jnp.einsum(
        "tf,ef->te", hidden_grad, expand_full, preferred_element_type=jnp.float32
    )
    mixed_grad = jnp.einsum("td,ed->te", upstream, project_full, preferred_element_type=jnp.float32)
    mixed_grad = mixed_grad.astype(jnp.bfloat16).reshape(seq_dev, seq_len, width)
    early_packed, mixed_grad = lax.optimization_barrier((early_packed, mixed_grad))
    expand_part, contract_part, project_part, inner_part, outer_part = scatter_columns(
        early_packed, early_widths
    )
    contract_part = contract_part.reshape(-1, width)
    inner_part = inner_part.reshape(-1)
    outer_part = outer_part.reshape(-1)
    backward_parts = [
        attention_backward(
            flat_query[s],
            flat_keys[s],
            flat_values[s],
            mixed_grad[s],
            forward_parts[s][1],
            forward_parts[s][2],
            lengths[s : s + 1],
        )
        for s in range(seq_dev)
    ]
    query_grad, key_grad, value_grad = (
        jnp.stack([part[j] for part in backward_parts]).reshape(seq_dev, seq_len, HEADS, HEAD_DIM)
        for j in range(3)
    )
    query_turned, key_turned = turn_pull((query_grad, key_grad))
    triple_grad = (
        jnp.stack([query_turned, key_turned, value_grad], axis=2)
        .reshape(positions, 3 * width)
        .astype(jnp.bfloat16)
    )
    attend_grad = jnp.einsum(
        "te,tc->ec", normed_low, triple_grad, preferred_element_type=jnp.float32
    )
    normed_grad = normed_grad + jnp.einsum(
        "tc,ec->te", triple_grad, attend_full, preferred_element_type=jnp.float32
    )
    rows_grad, gain_grad, shift_grad = norm_pull(normed_grad)
    token_grad = (
        (upstream.astype(jnp.float32) + rows_grad).astype(jnp.bfloat16).reshape(tokens.shape)
    )
    late = [
        attend_grad.astype(jnp.bfloat16),
        as_column(gain_grad.astype(jnp.bfloat16), rows_all),
        as_column(shift_grad.astype(jnp.bfloat16), rows_all),
    ]
    attend_part, gain_part, shift_part = scatter_columns(
        pad_columns(late), [block.shape[1] for block in late]
    )
    gain_part = gain_part.reshape(-1)
    shift_part = shift_part.reshape(-1)
    return (
        output,
        token_grad,
        attend_part,
        project_part,
        expand_part,
        contract_part,
        inner_part,
        outer_part,
        gain_part,
        shift_part,
    )


def solution(mesh):
    return jax.shard_map(
        body,
        mesh=mesh,
        in_specs=(
            P(("dp", "fsdp"), None, None),
            P(("dp", "fsdp")),
            P(("dp", "fsdp"), None),
            P(("dp", "fsdp"), None),
            P(("dp", "fsdp"), None),
            P(("dp", "fsdp"), None),
            P(("dp", "fsdp")),
            P(("dp", "fsdp")),
            P(("dp", "fsdp")),
            P(("dp", "fsdp")),
            P(("dp", "fsdp"), None, None),
        ),
        out_specs=(
            P(("dp", "fsdp"), None, None),
            P(("dp", "fsdp"), None, None),
            P(("dp", "fsdp"), None),
            P(("dp", "fsdp"), None),
            P(("dp", "fsdp"), None),
            P(("dp", "fsdp"), None),
            P(("dp", "fsdp")),
            P(("dp", "fsdp")),
            P(("dp", "fsdp")),
            P(("dp", "fsdp")),
        ),
        check_vma=False,
    )
```

```python
import math

import jax
import jax.numpy as jnp
from jax import lax
from jax.experimental import pallas as pl
from jax.experimental.pallas import tpu as pltpu
from jax.sharding import PartitionSpec as P


HEADS = 16
HEAD_DIM = 64
ROT = 32


epsilon = 1e-05


def layer_norm(rows, gain, shift):
    center = jnp.mean(rows, axis=-1, keepdims=True)
    spread = rows - center
    variance = jnp.mean(spread * spread, axis=-1, keepdims=True)
    return spread * lax.rsqrt(variance + epsilon) * gain + shift


def rotary_tables(length):
    position = jnp.arange(length).astype(jnp.float32)[:, None]
    ladder = jnp.arange(ROT // 2).astype(jnp.float32) * (-2.0 * math.log(10000.0) / ROT)
    angle = position * jnp.exp(ladder)[None, :]
    return (jnp.cos(angle)[:, None, :], jnp.sin(angle)[:, None, :])


def rotate(field, cosine, sine):
    paired = field[..., :ROT].reshape(field.shape[:-1] + (ROT // 2, 2))
    first = paired[..., 0]
    second = paired[..., 1]
    turned = jnp.stack([first * cosine - second * sine, second * cosine + first * sine], axis=-1)
    return jnp.concatenate([turned.reshape(field.shape[:-1] + (ROT,)), field[..., ROT:]], axis=-1)


QUERY_BLOCK = 256
NT = (((1,), (1,)), ((), ()))
TN = (((0,), (0,)), ((), ()))


def head_scores(q, k, first, length, lane_mask):
    scores = lax.dot_general(
        jnp.where(lane_mask, q, jnp.zeros_like(q)), k, NT, preferred_element_type=jnp.float32
    ) * HEAD_DIM ** (-0.5)
    query_place = first + lax.broadcasted_iota(jnp.int32, scores.shape, 0)
    key_place = lax.broadcasted_iota(jnp.int32, scores.shape, 1)
    allowed = (key_place <= query_place) & (key_place < length)
    return jnp.where(allowed, scores, -1000000000.0)


def attention_forward_kernel(length_ref, q_ref, k_ref, v_ref, o_ref, top_ref, total_ref):
    block = q_ref.shape[0]
    first = pl.program_id(1) * block
    length = length_ref[0]
    q = q_ref[...]
    k = k_ref[...]
    v = v_ref[...]
    lanes = lax.broadcasted_iota(jnp.int32, q.shape, 1)
    result = None
    for head in range(2):
        lane_mask = (lanes >= head * HEAD_DIM) & (lanes < (head + 1) * HEAD_DIM)
        masked = head_scores(q, k, first, length, lane_mask)
        top = jnp.max(masked, axis=-1, keepdims=True)
        weights = jnp.exp(masked - top)
        total = jnp.sum(weights, axis=-1, keepdims=True)
        probs = (weights / total).astype(jnp.bfloat16)
        out = jnp.dot(probs, v, preferred_element_type=jnp.float32)
        result = out if result is None else jnp.where(lane_mask, out, result)
        top_ref[head] = top
        total_ref[head] = total
    o_ref[...] = result.astype(o_ref.dtype)


def attention_backward_kernel(
    length_ref, q_ref, k_ref, v_ref, g_ref, top_ref, total_ref, dq_ref, dk_ref, dv_ref
):
    block = q_ref.shape[0]
    step = pl.program_id(1)
    first = step * block
    length = length_ref[0]
    scale = HEAD_DIM ** (-0.5)

    @pl.when(step == 0)
    def _():
        dk_ref[...] = jnp.zeros_like(dk_ref)
        dv_ref[...] = jnp.zeros_like(dv_ref)

    q = q_ref[...]
    k = k_ref[...]
    v = v_ref[...]
    g = g_ref[...]
    lanes = lax.broadcasted_iota(jnp.int32, q.shape, 1)
    key_lanes = lax.broadcasted_iota(jnp.int32, k.shape, 1)
    dq = None
    dk = None
    dv = None
    for head in range(2):
        lane_mask = (lanes >= head * HEAD_DIM) & (lanes < (head + 1) * HEAD_DIM)
        key_mask = (key_lanes >= head * HEAD_DIM) & (key_lanes < (head + 1) * HEAD_DIM)
        masked = head_scores(q, k, first, length, lane_mask)
        probs = jnp.exp(masked - top_ref[head]) / total_ref[head]
        upward = lax.dot_general(
            jnp.where(lane_mask, g, jnp.zeros_like(g)), v, NT, preferred_element_type=jnp.float32
        )
        inner = jnp.sum(probs * upward, axis=-1, keepdims=True)
        score_grad = (probs * (upward - inner)).astype(jnp.bfloat16)
        dq_head = jnp.dot(score_grad, k, preferred_element_type=jnp.float32) * scale
        dk_head = lax.dot_general(score_grad, q, TN, preferred_element_type=jnp.float32) * scale
        dv_head = lax.dot_general(
            probs.astype(jnp.bfloat16), g, TN, preferred_element_type=jnp.float32
        )
        if dq is None:
            dq, dk, dv = dq_head, dk_head, dv_head
        else:
            dq = jnp.where(lane_mask, dq_head, dq)
            dk = jnp.where(key_mask, dk_head, dk)
            dv = jnp.where(key_mask, dv_head, dv)
    dq_ref[...] = dq
    dk_ref[...] += dk
    dv_ref[...] += dv


def attention_forward(q, k, v, length):
    seq, width = q.shape
    pairs = width // (2 * HEAD_DIM)
    block = min(QUERY_BLOCK, seq)
    grid = (pairs, seq // block)
    lane = 2 * HEAD_DIM
    return pl.pallas_call(
        attention_forward_kernel,
        out_shape=(
            jax.ShapeDtypeStruct((seq, width), jnp.bfloat16),
            jax.ShapeDtypeStruct((2 * pairs, seq, 1), jnp.float32),
            jax.ShapeDtypeStruct((2 * pairs, seq, 1), jnp.float32),
        ),
        grid_spec=pltpu.PrefetchScalarGridSpec(
            num_scalar_prefetch=1,
            grid=grid,
            in_specs=[
                pl.BlockSpec((block, lane), lambda p, i, n: (i, p)),
                pl.BlockSpec((seq, lane), lambda p, i, n: (0, p)),
                pl.BlockSpec((seq, lane), lambda p, i, n: (0, p)),
            ],
            out_specs=[
                pl.BlockSpec((block, lane), lambda p, i, n: (i, p)),
                pl.BlockSpec((2, block, 1), lambda p, i, n: (p, i, 0)),
                pl.BlockSpec((2, block, 1), lambda p, i, n: (p, i, 0)),
            ],
        ),
        compiler_params=pltpu.CompilerParams(dimension_semantics=("parallel", "arbitrary")),
        cost_estimate=pl.CostEstimate(
            flops=8 * seq * seq * width, transcendentals=seq * seq * pairs * 2,
            bytes_accessed=2 * seq * width * 2 * (1 + 2 * seq // block),
        ),
    )(length, q, k, v)


def attention_backward(q, k, v, g, top, total, length):
    seq, width = q.shape
    pairs = width // (2 * HEAD_DIM)
    block = min(QUERY_BLOCK, seq)
    grid = (pairs, seq // block)
    lane = 2 * HEAD_DIM
    return pl.pallas_call(
        attention_backward_kernel,
        out_shape=(
            jax.ShapeDtypeStruct((seq, width), jnp.float32),
            jax.ShapeDtypeStruct((seq, width), jnp.float32),
            jax.ShapeDtypeStruct((seq, width), jnp.float32),
        ),
        grid_spec=pltpu.PrefetchScalarGridSpec(
            num_scalar_prefetch=1,
            grid=grid,
            in_specs=[
                pl.BlockSpec((block, lane), lambda p, i, n: (i, p)),
                pl.BlockSpec((seq, lane), lambda p, i, n: (0, p)),
                pl.BlockSpec((seq, lane), lambda p, i, n: (0, p)),
                pl.BlockSpec((block, lane), lambda p, i, n: (i, p)),
                pl.BlockSpec((2, block, 1), lambda p, i, n: (p, i, 0)),
                pl.BlockSpec((2, block, 1), lambda p, i, n: (p, i, 0)),
            ],
            out_specs=[
                pl.BlockSpec((block, lane), lambda p, i, n: (i, p)),
                pl.BlockSpec((seq, lane), lambda p, i, n: (0, p)),
                pl.BlockSpec((seq, lane), lambda p, i, n: (0, p)),
            ],
        ),
        compiler_params=pltpu.CompilerParams(dimension_semantics=("parallel", "arbitrary")),
        cost_estimate=pl.CostEstimate(
            flops=20 * seq * seq * width, transcendentals=seq * seq * pairs * 2,
            bytes_accessed=2 * seq * width * 2 * (2 + 2 * seq // block) + 3 * seq * width * 4,
        ),
    )(length, q, k, v, g, top, total)


def gelu_tanh(inner):
    return jax.nn.gelu(inner, approximate=True)


ALL = ("dp", "fsdp")


COLUMNS = 384


def pad_columns(blocks):
    width = sum(block.shape[1] for block in blocks)
    extra = -width % COLUMNS
    if extra:
        blocks = blocks + [jnp.zeros((blocks[0].shape[0], extra), blocks[0].dtype)]
    return jnp.concatenate(blocks, axis=1)


def split_columns(packed, widths):
    pieces = []
    offset = 0
    for width in widths:
        pieces.append(packed[:, offset : offset + width])
        offset += width
    return pieces


def gather_columns(blocks):
    packed = pad_columns(blocks)
    full = lax.all_gather(packed[None], ALL, axis=0, tiled=True)
    full = full.reshape(full.shape[0] * full.shape[1], full.shape[2])
    return split_columns(full, [block.shape[1] for block in blocks])


def scatter_columns(packed, widths):
    summed = lax.psum_scatter(packed, ALL, scatter_dimension=0, tiled=True)
    return [piece.astype(jnp.float32) for piece in split_columns(summed, widths)]


def as_column(vector, rows):
    return vector.reshape(rows, -1)


def body(
    tokens,
    lengths,
    attend_weight,
    project_weight,
    expand_weight,
    contract_weight,
    inner_bias,
    outer_bias,
    norm_gain,
    norm_shift,
    cotangent,
):
    seq_dev, seq_len, width = tokens.shape
    positions = seq_dev * seq_len
    rows_dev = attend_weight.shape[0]
    attend_full, gain_full, shift_full, inner_full, outer_full = gather_columns(
        [
            attend_weight,
            as_column(norm_gain, rows_dev),
            as_column(norm_shift, rows_dev),
            as_column(inner_bias, rows_dev),
            as_column(outer_bias, rows_dev),
        ]
    )
    gain_full = gain_full.reshape(-1)
    shift_full = shift_full.reshape(-1)
    inner_full = inner_full.reshape(-1)
    outer_full = outer_full.reshape(-1)
    expand_full, project_full, contract_full = gather_columns(
        [expand_weight, project_weight, contract_weight.reshape(rows_dev, -1)]
    )
    contract_full = contract_full.reshape(-1, width)
    rows = tokens.reshape(positions, width).astype(jnp.float32)
    normed, norm_pull = jax.vjp(
        layer_norm, rows, gain_full.astype(jnp.float32), shift_full.astype(jnp.float32)
    )
    normed_low = normed.astype(jnp.bfloat16)
    triple = jnp.dot(normed_low, attend_full, preferred_element_type=jnp.float32).reshape(
        seq_dev, seq_len, 3, HEADS, HEAD_DIM
    )
    cosine, sine = rotary_tables(seq_len)

    def turn(query, keys):
        return (rotate(query, cosine, sine), rotate(keys, cosine, sine))

    (query, keys), turn_pull = jax.vjp(turn, triple[:, :, 0], triple[:, :, 1])
    query_low = query.astype(jnp.bfloat16)
    keys_low = keys.astype(jnp.bfloat16)
    values_low = triple[:, :, 2].astype(jnp.bfloat16)
    flat_query = query_low.reshape(seq_dev, seq_len, width)
    flat_keys = keys_low.reshape(seq_dev, seq_len, width)
    flat_values = values_low.reshape(seq_dev, seq_len, width)
    forward_parts = [
        attention_forward(flat_query[s], flat_keys[s], flat_values[s], lengths[s : s + 1])
        for s in range(seq_dev)
    ]
    mixed_low = jnp.concatenate([part[0] for part in forward_parts], axis=0)
    hidden = jnp.dot(
        normed_low, expand_full, preferred_element_type=jnp.float32
    ) + inner_full.astype(jnp.float32)
    active, gelu_pull = jax.vjp(gelu_tanh, hidden)
    active_low = active.astype(jnp.bfloat16)
    result = rows + jnp.dot(mixed_low, project_full, preferred_element_type=jnp.float32)
    result = (
        result
        + jnp.dot(active_low, contract_full, preferred_element_type=jnp.float32)
        + outer_full.astype(jnp.float32)
    )
    output = result.astype(jnp.bfloat16).reshape(tokens.shape)
    upstream = cotangent.reshape(positions, width)
    contract_grad = jnp.einsum(
        "tf,td->fd", active_low, upstream, preferred_element_type=jnp.float32
    )
    rows_all = normed_low.shape[1]
    first = [contract_grad.astype(jnp.bfloat16).reshape(rows_all, -1)]
    first_packed = pad_columns(first)
    first_packed, contract_back = lax.optimization_barrier((first_packed, contract_full))
    (contract_part,) = scatter_columns(first_packed, [block.shape[1] for block in first])
    outer_grad = jnp.sum(upstream, axis=0, dtype=jnp.float32)
    project_grad = jnp.einsum("te,td->ed", mixed_low, upstream, preferred_element_type=jnp.float32)
    active_grad = jnp.einsum(
        "td,fd->tf", upstream, contract_back, preferred_element_type=jnp.float32
    )
    hidden_grad = gelu_pull(active_grad)[0].astype(jnp.bfloat16)
    expand_grad = jnp.einsum(
        "te,tf->ef", normed_low, hidden_grad, preferred_element_type=jnp.float32
    )
    inner_grad = jnp.sum(hidden_grad, axis=0, dtype=jnp.float32)
    early = [
        expand_grad.astype(jnp.bfloat16),
        project_grad.astype(jnp.bfloat16),
        as_column(inner_grad.astype(jnp.bfloat16), rows_all),
        as_column(outer_grad.astype(jnp.bfloat16), rows_all),
    ]
    early_widths = [block.shape[1] for block in early]
    early_packed = pad_columns(early)
    normed_grad = jnp.einsum(
        "tf,ef->te", hidden_grad, expand_full, preferred_element_type=jnp.float32
    )
    mixed_grad = jnp.einsum("td,ed->te", upstream, project_full, preferred_element_type=jnp.float32)
    mixed_grad = mixed_grad.astype(jnp.bfloat16).reshape(seq_dev, seq_len, width)
    early_packed, mixed_grad = lax.optimization_barrier((early_packed, mixed_grad))
    expand_part, project_part, inner_part, outer_part = scatter_columns(early_packed, early_widths)
    contract_part = contract_part.reshape(-1, width)
    inner_part = inner_part.reshape(-1)
    outer_part = outer_part.reshape(-1)
    backward_parts = [
        attention_backward(
            flat_query[s],
            flat_keys[s],
            flat_values[s],
            mixed_grad[s],
            forward_parts[s][1],
            forward_parts[s][2],
            lengths[s : s + 1],
        )
        for s in range(seq_dev)
    ]
    query_grad, key_grad, value_grad = (
        jnp.stack([part[j] for part in backward_parts]).reshape(seq_dev, seq_len, HEADS, HEAD_DIM)
        for j in range(3)
    )
    query_turned, key_turned = turn_pull((query_grad, key_grad))
    triple_grad = (
        jnp.stack([query_turned, key_turned, value_grad], axis=2)
        .reshape(positions, 3 * width)
        .astype(jnp.bfloat16)
    )
    attend_grad = jnp.einsum(
        "te,tc->ec", normed_low, triple_grad, preferred_element_type=jnp.float32
    )
    normed_grad = normed_grad + jnp.einsum(
        "tc,ec->te", triple_grad, attend_full, preferred_element_type=jnp.float32
    )
    rows_grad, gain_grad, shift_grad = norm_pull(normed_grad)
    token_grad = (
        (upstream.astype(jnp.float32) + rows_grad).astype(jnp.bfloat16).reshape(tokens.shape)
    )
    late = [
        attend_grad.astype(jnp.bfloat16),
        as_column(gain_grad.astype(jnp.bfloat16), rows_all),
        as_column(shift_grad.astype(jnp.bfloat16), rows_all),
    ]
    attend_part, gain_part, shift_part = scatter_columns(
        pad_columns(late), [block.shape[1] for block in late]
    )
    gain_part = gain_part.reshape(-1)
    shift_part = shift_part.reshape(-1)
    return (
        output,
        token_grad,
        attend_part,
        project_part,
        expand_part,
        contract_part,
        inner_part,
        outer_part,
        gain_part,
        shift_part,
    )


def solution(mesh):
    return jax.shard_map(
        body,
        mesh=mesh,
        in_specs=(
            P(("dp", "fsdp"), None, None),
            P(("dp", "fsdp")),
            P(("dp", "fsdp"), None),
            P(("dp", "fsdp"), None),
            P(("dp", "fsdp"), None),
            P(("dp", "fsdp"), None),
            P(("dp", "fsdp")),
            P(("dp", "fsdp")),
            P(("dp", "fsdp")),
            P(("dp", "fsdp")),
            P(("dp", "fsdp"), None, None),
        ),
        out_specs=(
            P(("dp", "fsdp"), None, None),
            P(("dp", "fsdp"), None, None),
            P(("dp", "fsdp"), None),
            P(("dp", "fsdp"), None),
            P(("dp", "fsdp"), None),
            P(("dp", "fsdp"), None),
            P(("dp", "fsdp")),
            P(("dp", "fsdp")),
            P(("dp", "fsdp")),
            P(("dp", "fsdp")),
        ),
        check_vma=False,
    )
```

```python
import math

import jax
import jax.numpy as jnp
from jax import lax
from jax.experimental import pallas as pl
from jax.experimental.pallas import tpu as pltpu
from jax.sharding import PartitionSpec as P


HEADS = 16
HEAD_DIM = 64
ROT = 32


epsilon = 1e-05


def layer_norm(rows, gain, shift):
    center = jnp.mean(rows, axis=-1, keepdims=True)
    spread = rows - center
    variance = jnp.mean(spread * spread, axis=-1, keepdims=True)
    return spread * lax.rsqrt(variance + epsilon) * gain + shift


def rotary_tables(length):
    position = jnp.arange(length).astype(jnp.float32)[:, None]
    ladder = jnp.arange(ROT // 2).astype(jnp.float32) * (-2.0 * math.log(10000.0) / ROT)
    angle = position * jnp.exp(ladder)[None, :]
    return (jnp.cos(angle)[:, None, :], jnp.sin(angle)[:, None, :])


def rotate(field, cosine, sine):
    paired = field[..., :ROT].reshape(field.shape[:-1] + (ROT // 2, 2))
    first = paired[..., 0]
    second = paired[..., 1]
    turned = jnp.stack([first * cosine - second * sine, second * cosine + first * sine], axis=-1)
    return jnp.concatenate([turned.reshape(field.shape[:-1] + (ROT,)), field[..., ROT:]], axis=-1)


QUERY_BLOCK = 256
NT = (((1,), (1,)), ((), ()))
TN = (((0,), (0,)), ((), ()))


def head_scores(q, k, first, length, lane_mask):
    scores = lax.dot_general(
        jnp.where(lane_mask, q, jnp.zeros_like(q)), k, NT, preferred_element_type=jnp.float32
    ) * HEAD_DIM ** (-0.5)
    query_place = first + lax.broadcasted_iota(jnp.int32, scores.shape, 0)
    key_place = lax.broadcasted_iota(jnp.int32, scores.shape, 1)
    allowed = (key_place <= query_place) & (key_place < length)
    return jnp.where(allowed, scores, -1000000000.0)


def attention_forward_kernel(length_ref, q_ref, k_ref, v_ref, o_ref, top_ref, total_ref):
    block = q_ref.shape[0]
    first = pl.program_id(1) * block
    length = length_ref[0]
    q = q_ref[...]
    k = k_ref[...]
    v = v_ref[...]
    lanes = lax.broadcasted_iota(jnp.int32, q.shape, 1)
    result = None
    for head in range(2):
        lane_mask = (lanes >= head * HEAD_DIM) & (lanes < (head + 1) * HEAD_DIM)
        masked = head_scores(q, k, first, length, lane_mask)
        top = jnp.max(masked, axis=-1, keepdims=True)
        weights = jnp.exp(masked - top)
        total = jnp.sum(weights, axis=-1, keepdims=True)
        probs = (weights / total).astype(jnp.bfloat16)
        out = jnp.dot(probs, v, preferred_element_type=jnp.float32)
        result = out if result is None else jnp.where(lane_mask, out, result)
        top_ref[head] = top
        total_ref[head] = total
    o_ref[...] = result.astype(o_ref.dtype)


def attention_backward_kernel(
    length_ref, q_ref, k_ref, v_ref, g_ref, top_ref, total_ref, dq_ref, dk_ref, dv_ref
):
    block = q_ref.shape[0]
    step = pl.program_id(1)
    first = step * block
    length = length_ref[0]
    scale = HEAD_DIM ** (-0.5)

    @pl.when(step == 0)
    def _():
        dk_ref[...] = jnp.zeros_like(dk_ref)
        dv_ref[...] = jnp.zeros_like(dv_ref)

    q = q_ref[...]
    k = k_ref[...]
    v = v_ref[...]
    g = g_ref[...]
    lanes = lax.broadcasted_iota(jnp.int32, q.shape, 1)
    key_lanes = lax.broadcasted_iota(jnp.int32, k.shape, 1)
    dq = None
    dk = None
    dv = None
    for head in range(2):
        lane_mask = (lanes >= head * HEAD_DIM) & (lanes < (head + 1) * HEAD_DIM)
        key_mask = (key_lanes >= head * HEAD_DIM) & (key_lanes < (head + 1) * HEAD_DIM)
        masked = head_scores(q, k, first, length, lane_mask)
        probs = jnp.exp(masked - top_ref[head]) / total_ref[head]
        upward = lax.dot_general(
            jnp.where(lane_mask, g, jnp.zeros_like(g)), v, NT, preferred_element_type=jnp.float32
        )
        inner = jnp.sum(probs * upward, axis=-1, keepdims=True)
        score_grad = (probs * (upward - inner)).astype(jnp.bfloat16)
        dq_head = jnp.dot(score_grad, k, preferred_element_type=jnp.float32) * scale
        dk_head = lax.dot_general(score_grad, q, TN, preferred_element_type=jnp.float32) * scale
        dv_head = lax.dot_general(
            probs.astype(jnp.bfloat16), g, TN, preferred_element_type=jnp.float32
        )
        if dq is None:
            dq, dk, dv = dq_head, dk_head, dv_head
        else:
            dq = jnp.where(lane_mask, dq_head, dq)
            dk = jnp.where(key_mask, dk_head, dk)
            dv = jnp.where(key_mask, dv_head, dv)
    dq_ref[...] = dq
    dk_ref[...] += dk
    dv_ref[...] += dv


def attention_forward(q, k, v, length):
    seq, width = q.shape
    pairs = width // (2 * HEAD_DIM)
    block = min(QUERY_BLOCK, seq)
    grid = (pairs, seq // block)
    lane = 2 * HEAD_DIM
    return pl.pallas_call(
        attention_forward_kernel,
        out_shape=(
            jax.ShapeDtypeStruct((seq, width), jnp.bfloat16),
            jax.ShapeDtypeStruct((2 * pairs, seq, 1), jnp.float32),
            jax.ShapeDtypeStruct((2 * pairs, seq, 1), jnp.float32),
        ),
        grid_spec=pltpu.PrefetchScalarGridSpec(
            num_scalar_prefetch=1,
            grid=grid,
            in_specs=[
                pl.BlockSpec((block, lane), lambda p, i, n: (i, p)),
                pl.BlockSpec((seq, lane), lambda p, i, n: (0, p)),
                pl.BlockSpec((seq, lane), lambda p, i, n: (0, p)),
            ],
            out_specs=[
                pl.BlockSpec((block, lane), lambda p, i, n: (i, p)),
                pl.BlockSpec((2, block, 1), lambda p, i, n: (p, i, 0)),
                pl.BlockSpec((2, block, 1), lambda p, i, n: (p, i, 0)),
            ],
        ),
        compiler_params=pltpu.CompilerParams(dimension_semantics=("parallel", "arbitrary")),
        cost_estimate=pl.CostEstimate(
            flops=8 * seq * seq * width, transcendentals=seq * seq * pairs * 2,
            bytes_accessed=2 * seq * width * 2 * (1 + 2 * seq // block),
        ),
    )(length, q, k, v)


def attention_backward(q, k, v, g, top, total, length):
    seq, width = q.shape
    pairs = width // (2 * HEAD_DIM)
    block = min(QUERY_BLOCK, seq)
    grid = (pairs, seq // block)
    lane = 2 * HEAD_DIM
    return pl.pallas_call(
        attention_backward_kernel,
        out_shape=(
            jax.ShapeDtypeStruct((seq, width), jnp.float32),
            jax.ShapeDtypeStruct((seq, width), jnp.float32),
            jax.ShapeDtypeStruct((seq, width), jnp.float32),
        ),
        grid_spec=pltpu.PrefetchScalarGridSpec(
            num_scalar_prefetch=1,
            grid=grid,
            in_specs=[
                pl.BlockSpec((block, lane), lambda p, i, n: (i, p)),
                pl.BlockSpec((seq, lane), lambda p, i, n: (0, p)),
                pl.BlockSpec((seq, lane), lambda p, i, n: (0, p)),
                pl.BlockSpec((block, lane), lambda p, i, n: (i, p)),
                pl.BlockSpec((2, block, 1), lambda p, i, n: (p, i, 0)),
                pl.BlockSpec((2, block, 1), lambda p, i, n: (p, i, 0)),
            ],
            out_specs=[
                pl.BlockSpec((block, lane), lambda p, i, n: (i, p)),
                pl.BlockSpec((seq, lane), lambda p, i, n: (0, p)),
                pl.BlockSpec((seq, lane), lambda p, i, n: (0, p)),
            ],
        ),
        compiler_params=pltpu.CompilerParams(dimension_semantics=("parallel", "arbitrary")),
        cost_estimate=pl.CostEstimate(
            flops=20 * seq * seq * width, transcendentals=seq * seq * pairs * 2,
            bytes_accessed=2 * seq * width * 2 * (2 + 2 * seq // block) + 3 * seq * width * 4,
        ),
    )(length, q, k, v, g, top, total)


def gelu_tanh(inner):
    return jax.nn.gelu(inner, approximate=True)


ALL = ("dp", "fsdp")


COLUMNS = 384


def pad_columns(blocks):
    width = sum(block.shape[1] for block in blocks)
    extra = -width % COLUMNS
    if extra:
        blocks = blocks + [jnp.zeros((blocks[0].shape[0], extra), blocks[0].dtype)]
    return jnp.concatenate(blocks, axis=1)


def split_columns(packed, widths):
    pieces = []
    offset = 0
    for width in widths:
        pieces.append(packed[:, offset : offset + width])
        offset += width
    return pieces


def gather_columns(blocks):
    packed = pad_columns(blocks)
    full = lax.all_gather(packed[None], ALL, axis=0, tiled=True)
    full = full.reshape(full.shape[0] * full.shape[1], full.shape[2])
    return split_columns(full, [block.shape[1] for block in blocks])


def scatter_columns(packed, widths):
    summed = lax.psum_scatter(packed, ALL, scatter_dimension=0, tiled=True)
    return [piece.astype(jnp.float32) for piece in split_columns(summed, widths)]


def as_column(vector, rows):
    return vector.reshape(rows, -1)


def body(
    tokens,
    lengths,
    attend_weight,
    project_weight,
    expand_weight,
    contract_weight,
    inner_bias,
    outer_bias,
    norm_gain,
    norm_shift,
    cotangent,
):
    seq_dev, seq_len, width = tokens.shape
    positions = seq_dev * seq_len
    rows_dev = attend_weight.shape[0]
    attend_full, gain_full, shift_full, inner_full, outer_full = gather_columns(
        [
            attend_weight,
            as_column(norm_gain, rows_dev),
            as_column(norm_shift, rows_dev),
            as_column(inner_bias, rows_dev),
            as_column(outer_bias, rows_dev),
        ],
    )
    gain_full = gain_full.reshape(-1)
    shift_full = shift_full.reshape(-1)
    inner_full = inner_full.reshape(-1)
    outer_full = outer_full.reshape(-1)
    expand_full, project_full = gather_columns([expand_weight, project_weight])
    (contract_full,) = gather_columns([contract_weight])
    rows = tokens.reshape(positions, width).astype(jnp.float32)
    normed, norm_pull = jax.vjp(
        layer_norm, rows, gain_full.astype(jnp.float32), shift_full.astype(jnp.float32)
    )
    normed_low = normed.astype(jnp.bfloat16)
    triple = jnp.dot(normed_low, attend_full, preferred_element_type=jnp.float32).reshape(
        seq_dev, seq_len, 3, HEADS, HEAD_DIM
    )
    cosine, sine = rotary_tables(seq_len)

    def turn(query, keys):
        return (rotate(query, cosine, sine), rotate(keys, cosine, sine))

    (query, keys), turn_pull = jax.vjp(turn, triple[:, :, 0], triple[:, :, 1])
    query_low = query.astype(jnp.bfloat16)
    keys_low = keys.astype(jnp.bfloat16)
    values_low = triple[:, :, 2].astype(jnp.bfloat16)
    flat_query = query_low.reshape(seq_dev, seq_len, width)
    flat_keys = keys_low.reshape(seq_dev, seq_len, width)
    flat_values = values_low.reshape(seq_dev, seq_len, width)
    forward_parts = [
        attention_forward(flat_query[s], flat_keys[s], flat_values[s], lengths[s : s + 1])
        for s in range(seq_dev)
    ]
    mixed_low = jnp.concatenate([part[0] for part in forward_parts], axis=0)
    hidden = jnp.dot(
        normed_low, expand_full, preferred_element_type=jnp.float32
    ) + inner_full.astype(jnp.float32)
    active, gelu_pull = jax.vjp(gelu_tanh, hidden)
    active_low = active.astype(jnp.bfloat16)
    result = rows + jnp.dot(mixed_low, project_full, preferred_element_type=jnp.float32)
    result = (
        result
        + jnp.dot(active_low, contract_full, preferred_element_type=jnp.float32)
        + outer_full.astype(jnp.float32)
    )
    output = result.astype(jnp.bfloat16).reshape(tokens.shape)
    upstream = cotangent.reshape(positions, width)
    contract_grad = jnp.einsum(
        "tf,td->fd", active_low, upstream, preferred_element_type=jnp.float32
    )
    rows_all = normed_low.shape[1]
    first = [contract_grad.astype(jnp.bfloat16)]
    first_packed = pad_columns(first)
    first_packed, upstream_back = lax.optimization_barrier((first_packed, upstream))
    (contract_part,) = scatter_columns(first_packed, [block.shape[1] for block in first])
    contract_part = contract_part.reshape(-1, width)
    outer_grad = jnp.sum(upstream_back, axis=0, dtype=jnp.float32)
    project_grad = jnp.einsum(
        "te,td->ed", mixed_low, upstream_back, preferred_element_type=jnp.float32
    )
    active_grad = jnp.einsum(
        "td,fd->tf", upstream_back, contract_full, preferred_element_type=jnp.float32
    )
    hidden_grad = gelu_pull(active_grad)[0].astype(jnp.bfloat16)
    expand_grad = jnp.einsum(
        "te,tf->ef", normed_low, hidden_grad, preferred_element_type=jnp.float32
    )
    inner_grad = jnp.sum(hidden_grad, axis=0, dtype=jnp.float32)
    early = [
        expand_grad.astype(jnp.bfloat16),
        project_grad.astype(jnp.bfloat16),
        as_column(inner_grad.astype(jnp.bfloat16), rows_all),
        as_column(outer_grad.astype(jnp.bfloat16), rows_all),
    ]
    early_widths = [block.shape[1] for block in early]
    early_packed = pad_columns(early)
    normed_grad = jnp.einsum(
        "tf,ef->te", hidden_grad, expand_full, preferred_element_type=jnp.float32
    )
    mixed_grad = jnp.einsum("td,ed->te", upstream, project_full, preferred_element_type=jnp.float32)
    mixed_grad = mixed_grad.astype(jnp.bfloat16).reshape(seq_dev, seq_len, width)
    early_packed, mixed_grad = lax.optimization_barrier((early_packed, mixed_grad))
    expand_part, project_part, inner_part, outer_part = scatter_columns(early_packed, early_widths)
    inner_part = inner_part.reshape(-1)
    outer_part = outer_part.reshape(-1)
    backward_parts = [
        attention_backward(
            flat_query[s],
            flat_keys[s],
            flat_values[s],
            mixed_grad[s],
            forward_parts[s][1],
            forward_parts[s][2],
            lengths[s : s + 1],
        )
        for s in range(seq_dev)
    ]
    query_grad, key_grad, value_grad = (
        jnp.stack([part[j] for part in backward_parts]).reshape(seq_dev, seq_len, HEADS, HEAD_DIM)
        for j in range(3)
    )
    query_turned, key_turned = turn_pull((query_grad, key_grad))
    triple_grad = (
        jnp.stack([query_turned, key_turned, value_grad], axis=2)
        .reshape(positions, 3 * width)
        .astype(jnp.bfloat16)
    )
    attend_grad = jnp.einsum(
        "te,tc->ec", normed_low, triple_grad, preferred_element_type=jnp.float32
    )
    normed_grad = normed_grad + jnp.einsum(
        "tc,ec->te", triple_grad, attend_full, preferred_element_type=jnp.float32
    )
    rows_grad, gain_grad, shift_grad = norm_pull(normed_grad)
    token_grad = (
        (upstream.astype(jnp.float32) + rows_grad).astype(jnp.bfloat16).reshape(tokens.shape)
    )
    late = [
        attend_grad.astype(jnp.bfloat16),
        as_column(gain_grad.astype(jnp.bfloat16), rows_all),
        as_column(shift_grad.astype(jnp.bfloat16), rows_all),
    ]
    attend_part, gain_part, shift_part = scatter_columns(
        pad_columns(late), [block.shape[1] for block in late]
    )
    gain_part = gain_part.reshape(-1)
    shift_part = shift_part.reshape(-1)
    return (
        output,
        token_grad,
        attend_part,
        project_part,
        expand_part,
        contract_part,
        inner_part,
        outer_part,
        gain_part,
        shift_part,
    )


def solution(mesh):
    return jax.shard_map(
        body,
        mesh=mesh,
        in_specs=(
            P(("dp", "fsdp"), None, None),
            P(("dp", "fsdp")),
            P(("dp", "fsdp"), None),
            P(("dp", "fsdp"), None),
            P(("dp", "fsdp"), None),
            P(("dp", "fsdp"), None),
            P(("dp", "fsdp")),
            P(("dp", "fsdp")),
            P(("dp", "fsdp")),
            P(("dp", "fsdp")),
            P(("dp", "fsdp"), None, None),
        ),
        out_specs=(
            P(("dp", "fsdp"), None, None),
            P(("dp", "fsdp"), None, None),
            P(("dp", "fsdp"), None),
            P(("dp", "fsdp"), None),
            P(("dp", "fsdp"), None),
            P(("dp", "fsdp"), None),
            P(("dp", "fsdp")),
            P(("dp", "fsdp")),
            P(("dp", "fsdp")),
            P(("dp", "fsdp")),
        ),
        check_vma=False,
    )
```

```python
import math

import jax
import jax.numpy as jnp
from jax import lax
from jax.experimental import pallas as pl
from jax.experimental.pallas import tpu as pltpu
from jax.sharding import PartitionSpec as P


HEADS = 16
HEAD_DIM = 64
ROT = 32


epsilon = 1e-05


def layer_norm(rows, gain, shift):
    center = jnp.mean(rows, axis=-1, keepdims=True)
    spread = rows - center
    variance = jnp.mean(spread * spread, axis=-1, keepdims=True)
    return spread * lax.rsqrt(variance + epsilon) * gain + shift


def rotary_tables(length):
    position = jnp.arange(length).astype(jnp.float32)[:, None]
    ladder = jnp.arange(ROT // 2).astype(jnp.float32) * (-2.0 * math.log(10000.0) / ROT)
    angle = position * jnp.exp(ladder)[None, :]
    return (jnp.cos(angle)[:, None, :], jnp.sin(angle)[:, None, :])


def rotate(field, cosine, sine):
    paired = field[..., :ROT].reshape(field.shape[:-1] + (ROT // 2, 2))
    first = paired[..., 0]
    second = paired[..., 1]
    turned = jnp.stack([first * cosine - second * sine, second * cosine + first * sine], axis=-1)
    return jnp.concatenate([turned.reshape(field.shape[:-1] + (ROT,)), field[..., ROT:]], axis=-1)


QUERY_BLOCK = 256
NT = (((1,), (1,)), ((), ()))
TN = (((0,), (0,)), ((), ()))


def head_scores(q, k, first, length, lane_mask):
    scores = lax.dot_general(
        jnp.where(lane_mask, q, jnp.zeros_like(q)), k, NT, preferred_element_type=jnp.float32
    ) * HEAD_DIM ** (-0.5)
    query_place = first + lax.broadcasted_iota(jnp.int32, scores.shape, 0)
    key_place = lax.broadcasted_iota(jnp.int32, scores.shape, 1)
    allowed = (key_place <= query_place) & (key_place < length)
    return jnp.where(allowed, scores, -1000000000.0)


def attention_forward_kernel(length_ref, q_ref, k_ref, v_ref, o_ref, top_ref, total_ref):
    block = q_ref.shape[0]
    first = pl.program_id(1) * block
    length = length_ref[0]
    q = q_ref[...]
    k = k_ref[...]
    v = v_ref[...]
    lanes = lax.broadcasted_iota(jnp.int32, q.shape, 1)
    result = None
    for head in range(2):
        lane_mask = (lanes >= head * HEAD_DIM) & (lanes < (head + 1) * HEAD_DIM)
        masked = head_scores(q, k, first, length, lane_mask)
        top = jnp.max(masked, axis=-1, keepdims=True)
        weights = jnp.exp(masked - top)
        total = jnp.sum(weights, axis=-1, keepdims=True)
        probs = (weights / total).astype(jnp.bfloat16)
        out = jnp.dot(probs, v, preferred_element_type=jnp.float32)
        result = out if result is None else jnp.where(lane_mask, out, result)
        top_ref[head] = top
        total_ref[head] = total
    o_ref[...] = result.astype(o_ref.dtype)


def attention_backward_kernel(
    length_ref, q_ref, k_ref, v_ref, g_ref, top_ref, total_ref, dq_ref, dk_ref, dv_ref
):
    block = q_ref.shape[0]
    step = pl.program_id(1)
    first = step * block
    length = length_ref[0]
    scale = HEAD_DIM ** (-0.5)

    @pl.when(step == 0)
    def _():
        dk_ref[...] = jnp.zeros_like(dk_ref)
        dv_ref[...] = jnp.zeros_like(dv_ref)

    q = q_ref[...]
    k = k_ref[...]
    v = v_ref[...]
    g = g_ref[...]
    lanes = lax.broadcasted_iota(jnp.int32, q.shape, 1)
    key_lanes = lax.broadcasted_iota(jnp.int32, k.shape, 1)
    dq = None
    dk = None
    dv = None
    for head in range(2):
        lane_mask = (lanes >= head * HEAD_DIM) & (lanes < (head + 1) * HEAD_DIM)
        key_mask = (key_lanes >= head * HEAD_DIM) & (key_lanes < (head + 1) * HEAD_DIM)
        masked = head_scores(q, k, first, length, lane_mask)
        probs = jnp.exp(masked - top_ref[head]) / total_ref[head]
        upward = lax.dot_general(
            jnp.where(lane_mask, g, jnp.zeros_like(g)), v, NT, preferred_element_type=jnp.float32
        )
        inner = jnp.sum(probs * upward, axis=-1, keepdims=True)
        score_grad = (probs * (upward - inner)).astype(jnp.bfloat16)
        dq_head = jnp.dot(score_grad, k, preferred_element_type=jnp.float32) * scale
        dk_head = lax.dot_general(score_grad, q, TN, preferred_element_type=jnp.float32) * scale
        dv_head = lax.dot_general(
            probs.astype(jnp.bfloat16), g, TN, preferred_element_type=jnp.float32
        )
        if dq is None:
            dq, dk, dv = dq_head, dk_head, dv_head
        else:
            dq = jnp.where(lane_mask, dq_head, dq)
            dk = jnp.where(key_mask, dk_head, dk)
            dv = jnp.where(key_mask, dv_head, dv)
    dq_ref[...] = dq
    dk_ref[...] += dk
    dv_ref[...] += dv


def attention_forward(q, k, v, length):
    seq, width = q.shape
    pairs = width // (2 * HEAD_DIM)
    block = min(QUERY_BLOCK, seq)
    grid = (pairs, seq // block)
    lane = 2 * HEAD_DIM
    return pl.pallas_call(
        attention_forward_kernel,
        out_shape=(
            jax.ShapeDtypeStruct((seq, width), jnp.bfloat16),
            jax.ShapeDtypeStruct((2 * pairs, seq, 1), jnp.float32),
            jax.ShapeDtypeStruct((2 * pairs, seq, 1), jnp.float32),
        ),
        grid_spec=pltpu.PrefetchScalarGridSpec(
            num_scalar_prefetch=1,
            grid=grid,
            in_specs=[
                pl.BlockSpec((block, lane), lambda p, i, n: (i, p)),
                pl.BlockSpec((seq, lane), lambda p, i, n: (0, p)),
                pl.BlockSpec((seq, lane), lambda p, i, n: (0, p)),
            ],
            out_specs=[
                pl.BlockSpec((block, lane), lambda p, i, n: (i, p)),
                pl.BlockSpec((2, block, 1), lambda p, i, n: (p, i, 0)),
                pl.BlockSpec((2, block, 1), lambda p, i, n: (p, i, 0)),
            ],
        ),
        compiler_params=pltpu.CompilerParams(dimension_semantics=("parallel", "arbitrary")),
        cost_estimate=pl.CostEstimate(
            flops=8 * seq * seq * width, transcendentals=seq * seq * pairs * 2,
            bytes_accessed=2 * seq * width * 2 * (1 + 2 * seq // block),
        ),
    )(length, q, k, v)


def attention_backward(q, k, v, g, top, total, length):
    seq, width = q.shape
    pairs = width // (2 * HEAD_DIM)
    block = min(QUERY_BLOCK, seq)
    grid = (pairs, seq // block)
    lane = 2 * HEAD_DIM
    return pl.pallas_call(
        attention_backward_kernel,
        out_shape=(
            jax.ShapeDtypeStruct((seq, width), jnp.float32),
            jax.ShapeDtypeStruct((seq, width), jnp.float32),
            jax.ShapeDtypeStruct((seq, width), jnp.float32),
        ),
        grid_spec=pltpu.PrefetchScalarGridSpec(
            num_scalar_prefetch=1,
            grid=grid,
            in_specs=[
                pl.BlockSpec((block, lane), lambda p, i, n: (i, p)),
                pl.BlockSpec((seq, lane), lambda p, i, n: (0, p)),
                pl.BlockSpec((seq, lane), lambda p, i, n: (0, p)),
                pl.BlockSpec((block, lane), lambda p, i, n: (i, p)),
                pl.BlockSpec((2, block, 1), lambda p, i, n: (p, i, 0)),
                pl.BlockSpec((2, block, 1), lambda p, i, n: (p, i, 0)),
            ],
            out_specs=[
                pl.BlockSpec((block, lane), lambda p, i, n: (i, p)),
                pl.BlockSpec((seq, lane), lambda p, i, n: (0, p)),
                pl.BlockSpec((seq, lane), lambda p, i, n: (0, p)),
            ],
        ),
        compiler_params=pltpu.CompilerParams(dimension_semantics=("parallel", "arbitrary")),
        cost_estimate=pl.CostEstimate(
            flops=20 * seq * seq * width, transcendentals=seq * seq * pairs * 2,
            bytes_accessed=2 * seq * width * 2 * (2 + 2 * seq // block) + 3 * seq * width * 4,
        ),
    )(length, q, k, v, g, top, total)


def gelu_tanh(inner):
    return jax.nn.gelu(inner, approximate=True)


ALL = ("dp", "fsdp")


COLUMNS = 384


def pad_columns(blocks):
    width = sum(block.shape[1] for block in blocks)
    extra = -width % COLUMNS
    if extra:
        blocks = blocks + [jnp.zeros((blocks[0].shape[0], extra), blocks[0].dtype)]
    return jnp.concatenate(blocks, axis=1)


def split_columns(packed, widths):
    pieces = []
    offset = 0
    for width in widths:
        pieces.append(packed[:, offset : offset + width])
        offset += width
    return pieces


def gather_columns(blocks):
    packed = pad_columns(blocks)
    full = lax.all_gather(packed[None], ALL, axis=0, tiled=True)
    full = full.reshape(full.shape[0] * full.shape[1], full.shape[2])
    return split_columns(full, [block.shape[1] for block in blocks])


def scatter_columns(packed, widths):
    summed = lax.psum_scatter(packed, ALL, scatter_dimension=0, tiled=True)
    return [piece.astype(jnp.float32) for piece in split_columns(summed, widths)]


def as_column(vector, rows):
    return vector.reshape(rows, -1)


def body(
    tokens,
    lengths,
    attend_weight,
    project_weight,
    expand_weight,
    contract_weight,
    inner_bias,
    outer_bias,
    norm_gain,
    norm_shift,
    cotangent,
):
    seq_dev, seq_len, width = tokens.shape
    positions = seq_dev * seq_len
    rows_dev = attend_weight.shape[0]
    expand_full, gain_full, shift_full, inner_full, outer_full = gather_columns(
        [
            expand_weight,
            as_column(norm_gain, rows_dev),
            as_column(norm_shift, rows_dev),
            as_column(inner_bias, rows_dev),
            as_column(outer_bias, rows_dev),
        ],
    )
    gain_full = gain_full.reshape(-1)
    shift_full = shift_full.reshape(-1)
    inner_full = inner_full.reshape(-1)
    outer_full = outer_full.reshape(-1)
    attend_full, project_full, contract_full = gather_columns(
        [attend_weight, project_weight, contract_weight.reshape(rows_dev, -1)]
    )
    contract_full = contract_full.reshape(-1, width)
    rows = tokens.reshape(positions, width).astype(jnp.float32)
    normed, norm_pull = jax.vjp(
        layer_norm, rows, gain_full.astype(jnp.float32), shift_full.astype(jnp.float32)
    )
    normed_low = normed.astype(jnp.bfloat16)
    upstream = cotangent.reshape(positions, width)
    hidden = jnp.dot(
        normed_low, expand_full, preferred_element_type=jnp.float32
    ) + inner_full.astype(jnp.float32)
    active, gelu_pull = jax.vjp(gelu_tanh, hidden)
    active_low = active.astype(jnp.bfloat16)
    contract_grad = jnp.einsum(
        "tf,td->fd", active_low, upstream, preferred_element_type=jnp.float32
    )
    rows_all = normed_low.shape[1]
    first = [contract_grad.astype(jnp.bfloat16)]
    first_packed = pad_columns(first)
    first_packed, upstream_back, attend_full = lax.optimization_barrier(
        (first_packed, upstream, attend_full)
    )
    (contract_part,) = scatter_columns(first_packed, [block.shape[1] for block in first])
    contract_part = contract_part.reshape(-1, width)
    triple = jnp.dot(normed_low, attend_full, preferred_element_type=jnp.float32)
    triple = triple.reshape(seq_dev, seq_len, 3, HEADS, HEAD_DIM)
    cosine, sine = rotary_tables(seq_len)

    def turn(query, keys):
        return (rotate(query, cosine, sine), rotate(keys, cosine, sine))

    (query, keys), turn_pull = jax.vjp(turn, triple[:, :, 0], triple[:, :, 1])
    query_low = query.astype(jnp.bfloat16)
    keys_low = keys.astype(jnp.bfloat16)
    values_low = triple[:, :, 2].astype(jnp.bfloat16)
    flat_query = query_low.reshape(seq_dev, seq_len, width)
    flat_keys = keys_low.reshape(seq_dev, seq_len, width)
    flat_values = values_low.reshape(seq_dev, seq_len, width)
    forward_parts = [
        attention_forward(flat_query[s], flat_keys[s], flat_values[s], lengths[s : s + 1])
        for s in range(seq_dev)
    ]
    mixed_low = jnp.concatenate([part[0] for part in forward_parts], axis=0)
    result = rows + jnp.dot(mixed_low, project_full, preferred_element_type=jnp.float32)
    result = (
        result
        + jnp.dot(active_low, contract_full, preferred_element_type=jnp.float32)
        + outer_full.astype(jnp.float32)
    )
    output = result.astype(jnp.bfloat16).reshape(tokens.shape)
    outer_grad = jnp.sum(upstream_back, axis=0, dtype=jnp.float32)
    project_grad = jnp.einsum(
        "te,td->ed", mixed_low, upstream_back, preferred_element_type=jnp.float32
    )
    active_grad = jnp.einsum(
        "td,fd->tf", upstream_back, contract_full, preferred_element_type=jnp.float32
    )
    hidden_grad = gelu_pull(active_grad)[0].astype(jnp.bfloat16)
    expand_grad = jnp.einsum(
        "te,tf->ef", normed_low, hidden_grad, preferred_element_type=jnp.float32
    )
    inner_grad = jnp.sum(hidden_grad, axis=0, dtype=jnp.float32)
    early = [
        expand_grad.astype(jnp.bfloat16),
        project_grad.astype(jnp.bfloat16),
        as_column(inner_grad.astype(jnp.bfloat16), rows_all),
        as_column(outer_grad.astype(jnp.bfloat16), rows_all),
    ]
    early_widths = [block.shape[1] for block in early]
    early_packed = pad_columns(early)
    normed_grad = jnp.einsum(
        "tf,ef->te", hidden_grad, expand_full, preferred_element_type=jnp.float32
    )
    mixed_grad = jnp.einsum("td,ed->te", upstream, project_full, preferred_element_type=jnp.float32)
    mixed_grad = mixed_grad.astype(jnp.bfloat16).reshape(seq_dev, seq_len, width)
    early_packed, mixed_grad = lax.optimization_barrier((early_packed, mixed_grad))
    expand_part, project_part, inner_part, outer_part = scatter_columns(early_packed, early_widths)
    inner_part = inner_part.reshape(-1)
    outer_part = outer_part.reshape(-1)
    backward_parts = [
        attention_backward(
            flat_query[s],
            flat_keys[s],
            flat_values[s],
            mixed_grad[s],
            forward_parts[s][1],
            forward_parts[s][2],
            lengths[s : s + 1],
        )
        for s in range(seq_dev)
    ]
    query_grad, key_grad, value_grad = (
        jnp.stack([part[j] for part in backward_parts]).reshape(seq_dev, seq_len, HEADS, HEAD_DIM)
        for j in range(3)
    )
    query_turned, key_turned = turn_pull((query_grad, key_grad))
    triple_grad = (
        jnp.stack([query_turned, key_turned, value_grad], axis=2)
        .reshape(positions, 3 * width)
        .astype(jnp.bfloat16)
    )
    attend_grad = jnp.einsum(
        "te,tc->ec", normed_low, triple_grad, preferred_element_type=jnp.float32
    )
    normed_grad = normed_grad + jnp.einsum(
        "tc,ec->te", triple_grad, attend_full, preferred_element_type=jnp.float32
    )
    rows_grad, gain_grad, shift_grad = norm_pull(normed_grad)
    token_grad = (
        (upstream.astype(jnp.float32) + rows_grad).astype(jnp.bfloat16).reshape(tokens.shape)
    )
    late = [
        attend_grad.astype(jnp.bfloat16),
        as_column(gain_grad.astype(jnp.bfloat16), rows_all),
        as_column(shift_grad.astype(jnp.bfloat16), rows_all),
    ]
    attend_part, gain_part, shift_part = scatter_columns(
        pad_columns(late), [block.shape[1] for block in late]
    )
    gain_part = gain_part.reshape(-1)
    shift_part = shift_part.reshape(-1)
    return (
        output,
        token_grad,
        attend_part,
        project_part,
        expand_part,
        contract_part,
        inner_part,
        outer_part,
        gain_part,
        shift_part,
    )


def solution(mesh):
    return jax.shard_map(
        body,
        mesh=mesh,
        in_specs=(
            P(("dp", "fsdp"), None, None),
            P(("dp", "fsdp")),
            P(("dp", "fsdp"), None),
            P(("dp", "fsdp"), None),
            P(("dp", "fsdp"), None),
            P(("dp", "fsdp"), None),
            P(("dp", "fsdp")),
            P(("dp", "fsdp")),
            P(("dp", "fsdp")),
            P(("dp", "fsdp")),
            P(("dp", "fsdp"), None, None),
        ),
        out_specs=(
            P(("dp", "fsdp"), None, None),
            P(("dp", "fsdp"), None, None),
            P(("dp", "fsdp"), None),
            P(("dp", "fsdp"), None),
            P(("dp", "fsdp"), None),
            P(("dp", "fsdp"), None),
            P(("dp", "fsdp")),
            P(("dp", "fsdp")),
            P(("dp", "fsdp")),
            P(("dp", "fsdp")),
        ),
        check_vma=False,
    )
```

```python
import math

import jax
import jax.numpy as jnp
from jax import lax
from jax.experimental import pallas as pl
from jax.experimental.pallas import tpu as pltpu
from jax.sharding import PartitionSpec as P


HEADS = 16
HEAD_DIM = 64
ROT = 32


epsilon = 1e-05


def layer_norm(rows, gain, shift):
    center = jnp.mean(rows, axis=-1, keepdims=True)
    spread = rows - center
    variance = jnp.mean(spread * spread, axis=-1, keepdims=True)
    return spread * lax.rsqrt(variance + epsilon) * gain + shift


def rotary_tables(length):
    position = jnp.arange(length).astype(jnp.float32)[:, None]
    ladder = jnp.arange(ROT // 2).astype(jnp.float32) * (-2.0 * math.log(10000.0) / ROT)
    angle = position * jnp.exp(ladder)[None, :]
    return (jnp.cos(angle)[:, None, :], jnp.sin(angle)[:, None, :])


def rotate(field, cosine, sine):
    paired = field[..., :ROT].reshape(field.shape[:-1] + (ROT // 2, 2))
    first = paired[..., 0]
    second = paired[..., 1]
    turned = jnp.stack([first * cosine - second * sine, second * cosine + first * sine], axis=-1)
    return jnp.concatenate([turned.reshape(field.shape[:-1] + (ROT,)), field[..., ROT:]], axis=-1)


QUERY_BLOCK = 256
NT = (((1,), (1,)), ((), ()))
TN = (((0,), (0,)), ((), ()))


def head_scores(q, k, first, length, lane_mask):
    scores = lax.dot_general(
        jnp.where(lane_mask, q, jnp.zeros_like(q)), k, NT, preferred_element_type=jnp.float32
    ) * HEAD_DIM ** (-0.5)
    query_place = first + lax.broadcasted_iota(jnp.int32, scores.shape, 0)
    key_place = lax.broadcasted_iota(jnp.int32, scores.shape, 1)
    allowed = (key_place <= query_place) & (key_place < length)
    return jnp.where(allowed, scores, -1000000000.0)


def attention_forward_kernel(length_ref, q_ref, k_ref, v_ref, o_ref, top_ref, total_ref):
    block = q_ref.shape[0]
    first = pl.program_id(1) * block
    length = length_ref[0]
    q = q_ref[...]
    k = k_ref[...]
    v = v_ref[...]
    lanes = lax.broadcasted_iota(jnp.int32, q.shape, 1)
    result = None
    for head in range(2):
        lane_mask = (lanes >= head * HEAD_DIM) & (lanes < (head + 1) * HEAD_DIM)
        masked = head_scores(q, k, first, length, lane_mask)
        top = jnp.max(masked, axis=-1, keepdims=True)
        weights = jnp.exp(masked - top)
        total = jnp.sum(weights, axis=-1, keepdims=True)
        probs = (weights / total).astype(jnp.bfloat16)
        out = jnp.dot(probs, v, preferred_element_type=jnp.float32)
        result = out if result is None else jnp.where(lane_mask, out, result)
        top_ref[head] = top
        total_ref[head] = total
    o_ref[...] = result.astype(o_ref.dtype)


def attention_backward_kernel(
    length_ref, q_ref, k_ref, v_ref, g_ref, top_ref, total_ref, dq_ref, dk_ref, dv_ref
):
    block = q_ref.shape[0]
    step = pl.program_id(1)
    first = step * block
    length = length_ref[0]
    scale = HEAD_DIM ** (-0.5)

    @pl.when(step == 0)
    def _():
        dk_ref[...] = jnp.zeros_like(dk_ref)
        dv_ref[...] = jnp.zeros_like(dv_ref)

    q = q_ref[...]
    k = k_ref[...]
    v = v_ref[...]
    g = g_ref[...]
    lanes = lax.broadcasted_iota(jnp.int32, q.shape, 1)
    key_lanes = lax.broadcasted_iota(jnp.int32, k.shape, 1)
    dq = None
    dk = None
    dv = None
    for head in range(2):
        lane_mask = (lanes >= head * HEAD_DIM) & (lanes < (head + 1) * HEAD_DIM)
        key_mask = (key_lanes >= head * HEAD_DIM) & (key_lanes < (head + 1) * HEAD_DIM)
        masked = head_scores(q, k, first, length, lane_mask)
        probs = jnp.exp(masked - top_ref[head]) / total_ref[head]
        upward = lax.dot_general(
            jnp.where(lane_mask, g, jnp.zeros_like(g)), v, NT, preferred_element_type=jnp.float32
        )
        inner = jnp.sum(probs * upward, axis=-1, keepdims=True)
        score_grad = (probs * (upward - inner)).astype(jnp.bfloat16)
        dq_head = jnp.dot(score_grad, k, preferred_element_type=jnp.float32) * scale
        dk_head = lax.dot_general(score_grad, q, TN, preferred_element_type=jnp.float32) * scale
        dv_head = lax.dot_general(
            probs.astype(jnp.bfloat16), g, TN, preferred_element_type=jnp.float32
        )
        if dq is None:
            dq, dk, dv = dq_head, dk_head, dv_head
        else:
            dq = jnp.where(lane_mask, dq_head, dq)
            dk = jnp.where(key_mask, dk_head, dk)
            dv = jnp.where(key_mask, dv_head, dv)
    dq_ref[...] = dq
    dk_ref[...] += dk
    dv_ref[...] += dv


def attention_forward(q, k, v, length):
    seq, width = q.shape
    pairs = width // (2 * HEAD_DIM)
    block = min(QUERY_BLOCK, seq)
    grid = (pairs, seq // block)
    lane = 2 * HEAD_DIM
    return pl.pallas_call(
        attention_forward_kernel,
        out_shape=(
            jax.ShapeDtypeStruct((seq, width), jnp.bfloat16),
            jax.ShapeDtypeStruct((2 * pairs, seq, 1), jnp.float32),
            jax.ShapeDtypeStruct((2 * pairs, seq, 1), jnp.float32),
        ),
        grid_spec=pltpu.PrefetchScalarGridSpec(
            num_scalar_prefetch=1,
            grid=grid,
            in_specs=[
                pl.BlockSpec((block, lane), lambda p, i, n: (i, p)),
                pl.BlockSpec((seq, lane), lambda p, i, n: (0, p)),
                pl.BlockSpec((seq, lane), lambda p, i, n: (0, p)),
            ],
            out_specs=[
                pl.BlockSpec((block, lane), lambda p, i, n: (i, p)),
                pl.BlockSpec((2, block, 1), lambda p, i, n: (p, i, 0)),
                pl.BlockSpec((2, block, 1), lambda p, i, n: (p, i, 0)),
            ],
        ),
        compiler_params=pltpu.CompilerParams(dimension_semantics=("parallel", "arbitrary")),
        cost_estimate=pl.CostEstimate(
            flops=8 * seq * seq * width, transcendentals=seq * seq * pairs * 2,
            bytes_accessed=2 * seq * width * 2 * (1 + 2 * seq // block),
        ),
    )(length, q, k, v)


def attention_backward(q, k, v, g, top, total, length):
    seq, width = q.shape
    pairs = width // (2 * HEAD_DIM)
    block = min(QUERY_BLOCK, seq)
    grid = (pairs, seq // block)
    lane = 2 * HEAD_DIM
    return pl.pallas_call(
        attention_backward_kernel,
        out_shape=(
            jax.ShapeDtypeStruct((seq, width), jnp.float32),
            jax.ShapeDtypeStruct((seq, width), jnp.float32),
            jax.ShapeDtypeStruct((seq, width), jnp.float32),
        ),
        grid_spec=pltpu.PrefetchScalarGridSpec(
            num_scalar_prefetch=1,
            grid=grid,
            in_specs=[
                pl.BlockSpec((block, lane), lambda p, i, n: (i, p)),
                pl.BlockSpec((seq, lane), lambda p, i, n: (0, p)),
                pl.BlockSpec((seq, lane), lambda p, i, n: (0, p)),
                pl.BlockSpec((block, lane), lambda p, i, n: (i, p)),
                pl.BlockSpec((2, block, 1), lambda p, i, n: (p, i, 0)),
                pl.BlockSpec((2, block, 1), lambda p, i, n: (p, i, 0)),
            ],
            out_specs=[
                pl.BlockSpec((block, lane), lambda p, i, n: (i, p)),
                pl.BlockSpec((seq, lane), lambda p, i, n: (0, p)),
                pl.BlockSpec((seq, lane), lambda p, i, n: (0, p)),
            ],
        ),
        compiler_params=pltpu.CompilerParams(dimension_semantics=("parallel", "arbitrary")),
        cost_estimate=pl.CostEstimate(
            flops=20 * seq * seq * width, transcendentals=seq * seq * pairs * 2,
            bytes_accessed=2 * seq * width * 2 * (2 + 2 * seq // block) + 3 * seq * width * 4,
        ),
    )(length, q, k, v, g, top, total)


def gelu_tanh(inner):
    return jax.nn.gelu(inner, approximate=True)


ALL = ("dp", "fsdp")


COLUMNS = 384
GATHER_COLUMNS = 128


def pad_columns(blocks, multiple=COLUMNS):
    width = sum(block.shape[1] for block in blocks)
    extra = -width % multiple
    if extra:
        blocks = blocks + [jnp.zeros((blocks[0].shape[0], extra), blocks[0].dtype)]
    return jnp.concatenate(blocks, axis=1)


def split_columns(packed, widths):
    pieces = []
    offset = 0
    for width in widths:
        pieces.append(packed[:, offset : offset + width])
        offset += width
    return pieces


def gather_columns(blocks):
    packed = pad_columns(blocks, GATHER_COLUMNS)
    full = lax.all_gather(packed[None], ALL, axis=0, tiled=True)
    full = full.reshape(full.shape[0] * full.shape[1], full.shape[2])
    return split_columns(full, [block.shape[1] for block in blocks])


def scatter_columns(packed, widths):
    summed = lax.psum_scatter(packed, ALL, scatter_dimension=0, tiled=True)
    return [piece.astype(jnp.float32) for piece in split_columns(summed, widths)]


def as_column(vector, rows):
    return vector.reshape(rows, -1)


def body(
    tokens,
    lengths,
    attend_weight,
    project_weight,
    expand_weight,
    contract_weight,
    inner_bias,
    outer_bias,
    norm_gain,
    norm_shift,
    cotangent,
):
    seq_dev, seq_len, width = tokens.shape
    positions = seq_dev * seq_len
    rows_dev = attend_weight.shape[0]
    attend_full, gain_full, shift_full, inner_full, outer_full = gather_columns(
        [
            attend_weight,
            as_column(norm_gain, rows_dev),
            as_column(norm_shift, rows_dev),
            as_column(inner_bias, rows_dev),
            as_column(outer_bias, rows_dev),
        ],
    )
    gain_full = gain_full.reshape(-1)
    shift_full = shift_full.reshape(-1)
    inner_full = inner_full.reshape(-1)
    outer_full = outer_full.reshape(-1)
    expand_full, project_full = gather_columns([expand_weight, project_weight])
    (contract_full,) = gather_columns([contract_weight])
    rows = tokens.reshape(positions, width).astype(jnp.float32)
    normed, norm_pull = jax.vjp(
        layer_norm, rows, gain_full.astype(jnp.float32), shift_full.astype(jnp.float32)
    )
    normed_low = normed.astype(jnp.bfloat16)
    triple = jnp.dot(normed_low, attend_full, preferred_element_type=jnp.float32).reshape(
        seq_dev, seq_len, 3, HEADS, HEAD_DIM
    )
    cosine, sine = rotary_tables(seq_len)

    def turn(query, keys):
        return (rotate(query, cosine, sine), rotate(keys, cosine, sine))

    (query, keys), turn_pull = jax.vjp(turn, triple[:, :, 0], triple[:, :, 1])
    query_low = query.astype(jnp.bfloat16)
    keys_low = keys.astype(jnp.bfloat16)
    values_low = triple[:, :, 2].astype(jnp.bfloat16)
    flat_query = query_low.reshape(seq_dev, seq_len, width)
    flat_keys = keys_low.reshape(seq_dev, seq_len, width)
    flat_values = values_low.reshape(seq_dev, seq_len, width)
    forward_parts = [
        attention_forward(flat_query[s], flat_keys[s], flat_values[s], lengths[s : s + 1])
        for s in range(seq_dev)
    ]
    mixed_low = jnp.concatenate([part[0] for part in forward_parts], axis=0)
    hidden = jnp.dot(
        normed_low, expand_full, preferred_element_type=jnp.float32
    ) + inner_full.astype(jnp.float32)
    active, gelu_pull = jax.vjp(gelu_tanh, hidden)
    active_low = active.astype(jnp.bfloat16)
    result = rows + jnp.dot(mixed_low, project_full, preferred_element_type=jnp.float32)
    result = (
        result
        + jnp.dot(active_low, contract_full, preferred_element_type=jnp.float32)
        + outer_full.astype(jnp.float32)
    )
    output = result.astype(jnp.bfloat16).reshape(tokens.shape)
    upstream = cotangent.reshape(positions, width)
    contract_grad = jnp.einsum(
        "tf,td->fd", active_low, upstream, preferred_element_type=jnp.float32
    )
    rows_all = normed_low.shape[1]
    first = [contract_grad.astype(jnp.bfloat16)]
    first_packed = pad_columns(first)
    first_packed, upstream_back = lax.optimization_barrier((first_packed, upstream))
    (contract_part,) = scatter_columns(first_packed, [block.shape[1] for block in first])
    contract_part = contract_part.reshape(-1, width)
    outer_grad = jnp.sum(upstream_back, axis=0, dtype=jnp.float32)
    project_grad = jnp.einsum(
        "te,td->ed", mixed_low, upstream_back, preferred_element_type=jnp.float32
    )
    active_grad = jnp.einsum(
        "td,fd->tf", upstream_back, contract_full, preferred_element_type=jnp.float32
    )
    hidden_grad = gelu_pull(active_grad)[0].astype(jnp.bfloat16)
    expand_grad = jnp.einsum(
        "te,tf->ef", normed_low, hidden_grad, preferred_element_type=jnp.float32
    )
    inner_grad = jnp.sum(hidden_grad, axis=0, dtype=jnp.float32)
    early = [
        expand_grad.astype(jnp.bfloat16),
        as_column(inner_grad.astype(jnp.bfloat16), rows_all),
        as_column(outer_grad.astype(jnp.bfloat16), rows_all),
    ]
    early_widths = [block.shape[1] for block in early]
    early_packed = pad_columns(early)
    normed_grad = jnp.einsum(
        "tf,ef->te", hidden_grad, expand_full, preferred_element_type=jnp.float32
    )
    mixed_grad = jnp.einsum("td,ed->te", upstream, project_full, preferred_element_type=jnp.float32)
    mixed_grad = mixed_grad.astype(jnp.bfloat16).reshape(seq_dev, seq_len, width)
    early_packed, mixed_grad = lax.optimization_barrier((early_packed, mixed_grad))
    expand_part, inner_part, outer_part = scatter_columns(early_packed, early_widths)
    inner_part = inner_part.reshape(-1)
    outer_part = outer_part.reshape(-1)
    backward_parts = [
        attention_backward(
            flat_query[s],
            flat_keys[s],
            flat_values[s],
            mixed_grad[s],
            forward_parts[s][1],
            forward_parts[s][2],
            lengths[s : s + 1],
        )
        for s in range(seq_dev)
    ]
    query_grad, key_grad, value_grad = (
        jnp.stack([part[j] for part in backward_parts]).reshape(seq_dev, seq_len, HEADS, HEAD_DIM)
        for j in range(3)
    )
    query_turned, key_turned = turn_pull((query_grad, key_grad))
    triple_grad = (
        jnp.stack([query_turned, key_turned, value_grad], axis=2)
        .reshape(positions, 3 * width)
        .astype(jnp.bfloat16)
    )
    attend_grad = jnp.einsum(
        "te,tc->ec", normed_low, triple_grad, preferred_element_type=jnp.float32
    )
    normed_grad = normed_grad + jnp.einsum(
        "tc,ec->te", triple_grad, attend_full, preferred_element_type=jnp.float32
    )
    rows_grad, gain_grad, shift_grad = norm_pull(normed_grad)
    token_grad = (
        (upstream.astype(jnp.float32) + rows_grad).astype(jnp.bfloat16).reshape(tokens.shape)
    )
    late = [
        attend_grad.astype(jnp.bfloat16),
        project_grad.astype(jnp.bfloat16),
        as_column(gain_grad.astype(jnp.bfloat16), rows_all),
        as_column(shift_grad.astype(jnp.bfloat16), rows_all),
    ]
    attend_part, project_part, gain_part, shift_part = scatter_columns(
        pad_columns(late), [block.shape[1] for block in late]
    )
    gain_part = gain_part.reshape(-1)
    shift_part = shift_part.reshape(-1)
    return (
        output,
        token_grad,
        attend_part,
        project_part,
        expand_part,
        contract_part,
        inner_part,
        outer_part,
        gain_part,
        shift_part,
    )


def solution(mesh):
    return jax.shard_map(
        body,
        mesh=mesh,
        in_specs=(
            P(("dp", "fsdp"), None, None),
            P(("dp", "fsdp")),
            P(("dp", "fsdp"), None),
            P(("dp", "fsdp"), None),
            P(("dp", "fsdp"), None),
            P(("dp", "fsdp"), None),
            P(("dp", "fsdp")),
            P(("dp", "fsdp")),
            P(("dp", "fsdp")),
            P(("dp", "fsdp")),
            P(("dp", "fsdp"), None, None),
        ),
        out_specs=(
            P(("dp", "fsdp"), None, None),
            P(("dp", "fsdp"), None, None),
            P(("dp", "fsdp"), None),
            P(("dp", "fsdp"), None),
            P(("dp", "fsdp"), None),
            P(("dp", "fsdp"), None),
            P(("dp", "fsdp")),
            P(("dp", "fsdp")),
            P(("dp", "fsdp")),
            P(("dp", "fsdp")),
        ),
        check_vma=False,
    )
```

```python
import math

import jax
import jax.numpy as jnp
from jax import lax
from jax.experimental import pallas as pl
from jax.experimental.pallas import tpu as pltpu
from jax.sharding import PartitionSpec as P


HEADS = 16
HEAD_DIM = 64
ROT = 32


epsilon = 1e-05


def layer_norm(rows, gain, shift):
    center = jnp.mean(rows, axis=-1, keepdims=True)
    spread = rows - center
    variance = jnp.mean(spread * spread, axis=-1, keepdims=True)
    return spread * lax.rsqrt(variance + epsilon) * gain + shift


def rotary_tables(length):
    position = jnp.arange(length).astype(jnp.float32)[:, None]
    ladder = jnp.arange(ROT // 2).astype(jnp.float32) * (-2.0 * math.log(10000.0) / ROT)
    angle = position * jnp.exp(ladder)[None, :]
    return (jnp.cos(angle)[:, None, :], jnp.sin(angle)[:, None, :])


def rotate(field, cosine, sine):
    paired = field[..., :ROT].reshape(field.shape[:-1] + (ROT // 2, 2))
    first = paired[..., 0]
    second = paired[..., 1]
    turned = jnp.stack([first * cosine - second * sine, second * cosine + first * sine], axis=-1)
    return jnp.concatenate([turned.reshape(field.shape[:-1] + (ROT,)), field[..., ROT:]], axis=-1)


QUERY_BLOCK = 256
NT = (((1,), (1,)), ((), ()))
TN = (((0,), (0,)), ((), ()))


def head_scores(q, k, first, length, lane_mask):
    scores = lax.dot_general(
        jnp.where(lane_mask, q, jnp.zeros_like(q)), k, NT, preferred_element_type=jnp.float32
    ) * HEAD_DIM ** (-0.5)
    query_place = first + lax.broadcasted_iota(jnp.int32, scores.shape, 0)
    key_place = lax.broadcasted_iota(jnp.int32, scores.shape, 1)
    allowed = (key_place <= query_place) & (key_place < length)
    return jnp.where(allowed, scores, -1000000000.0)


def attention_forward_kernel(length_ref, q_ref, k_ref, v_ref, o_ref, top_ref, total_ref):
    block = q_ref.shape[0]
    first = pl.program_id(1) * block
    length = length_ref[0]
    q = q_ref[...]
    k = k_ref[...]
    v = v_ref[...]
    lanes = lax.broadcasted_iota(jnp.int32, q.shape, 1)
    result = None
    for head in range(2):
        lane_mask = (lanes >= head * HEAD_DIM) & (lanes < (head + 1) * HEAD_DIM)
        masked = head_scores(q, k, first, length, lane_mask)
        top = jnp.max(masked, axis=-1, keepdims=True)
        weights = jnp.exp(masked - top)
        total = jnp.sum(weights, axis=-1, keepdims=True)
        probs = (weights / total).astype(jnp.bfloat16)
        out = jnp.dot(probs, v, preferred_element_type=jnp.float32)
        result = out if result is None else jnp.where(lane_mask, out, result)
        top_ref[head] = top
        total_ref[head] = total
    o_ref[...] = result.astype(o_ref.dtype)


def attention_backward_kernel(
    length_ref, q_ref, k_ref, v_ref, g_ref, top_ref, total_ref, dq_ref, dk_ref, dv_ref
):
    block = q_ref.shape[0]
    step = pl.program_id(1)
    first = step * block
    length = length_ref[0]
    scale = HEAD_DIM ** (-0.5)

    @pl.when(step == 0)
    def _():
        dk_ref[...] = jnp.zeros_like(dk_ref)
        dv_ref[...] = jnp.zeros_like(dv_ref)

    q = q_ref[...]
    k = k_ref[...]
    v = v_ref[...]
    g = g_ref[...]
    lanes = lax.broadcasted_iota(jnp.int32, q.shape, 1)
    key_lanes = lax.broadcasted_iota(jnp.int32, k.shape, 1)
    dq = None
    dk = None
    dv = None
    for head in range(2):
        lane_mask = (lanes >= head * HEAD_DIM) & (lanes < (head + 1) * HEAD_DIM)
        key_mask = (key_lanes >= head * HEAD_DIM) & (key_lanes < (head + 1) * HEAD_DIM)
        masked = head_scores(q, k, first, length, lane_mask)
        probs = jnp.exp(masked - top_ref[head]) / total_ref[head]
        upward = lax.dot_general(
            jnp.where(lane_mask, g, jnp.zeros_like(g)), v, NT, preferred_element_type=jnp.float32
        )
        inner = jnp.sum(probs * upward, axis=-1, keepdims=True)
        score_grad = (probs * (upward - inner)).astype(jnp.bfloat16)
        dq_head = jnp.dot(score_grad, k, preferred_element_type=jnp.float32) * scale
        dk_head = lax.dot_general(score_grad, q, TN, preferred_element_type=jnp.float32) * scale
        dv_head = lax.dot_general(
            probs.astype(jnp.bfloat16), g, TN, preferred_element_type=jnp.float32
        )
        if dq is None:
            dq, dk, dv = dq_head, dk_head, dv_head
        else:
            dq = jnp.where(lane_mask, dq_head, dq)
            dk = jnp.where(key_mask, dk_head, dk)
            dv = jnp.where(key_mask, dv_head, dv)
    dq_ref[...] = dq
    dk_ref[...] += dk
    dv_ref[...] += dv


def attention_forward(q, k, v, length):
    seq, width = q.shape
    pairs = width // (2 * HEAD_DIM)
    block = min(QUERY_BLOCK, seq)
    grid = (pairs, seq // block)
    lane = 2 * HEAD_DIM
    return pl.pallas_call(
        attention_forward_kernel,
        out_shape=(
            jax.ShapeDtypeStruct((seq, width), jnp.bfloat16),
            jax.ShapeDtypeStruct((2 * pairs, seq, 1), jnp.float32),
            jax.ShapeDtypeStruct((2 * pairs, seq, 1), jnp.float32),
        ),
        grid_spec=pltpu.PrefetchScalarGridSpec(
            num_scalar_prefetch=1,
            grid=grid,
            in_specs=[
                pl.BlockSpec((block, lane), lambda p, i, n: (i, p)),
                pl.BlockSpec((seq, lane), lambda p, i, n: (0, p)),
                pl.BlockSpec((seq, lane), lambda p, i, n: (0, p)),
            ],
            out_specs=[
                pl.BlockSpec((block, lane), lambda p, i, n: (i, p)),
                pl.BlockSpec((2, block, 1), lambda p, i, n: (p, i, 0)),
                pl.BlockSpec((2, block, 1), lambda p, i, n: (p, i, 0)),
            ],
        ),
        compiler_params=pltpu.CompilerParams(dimension_semantics=("parallel", "arbitrary")),
        cost_estimate=pl.CostEstimate(
            flops=8 * seq * seq * width, transcendentals=seq * seq * pairs * 2,
            bytes_accessed=2 * seq * width * 2 * (1 + 2 * seq // block),
        ),
    )(length, q, k, v)


def attention_backward(q, k, v, g, top, total, length):
    seq, width = q.shape
    pairs = width // (2 * HEAD_DIM)
    block = min(QUERY_BLOCK, seq)
    grid = (pairs, seq // block)
    lane = 2 * HEAD_DIM
    return pl.pallas_call(
        attention_backward_kernel,
        out_shape=(
            jax.ShapeDtypeStruct((seq, width), jnp.float32),
            jax.ShapeDtypeStruct((seq, width), jnp.float32),
            jax.ShapeDtypeStruct((seq, width), jnp.float32),
        ),
        grid_spec=pltpu.PrefetchScalarGridSpec(
            num_scalar_prefetch=1,
            grid=grid,
            in_specs=[
                pl.BlockSpec((block, lane), lambda p, i, n: (i, p)),
                pl.BlockSpec((seq, lane), lambda p, i, n: (0, p)),
                pl.BlockSpec((seq, lane), lambda p, i, n: (0, p)),
                pl.BlockSpec((block, lane), lambda p, i, n: (i, p)),
                pl.BlockSpec((2, block, 1), lambda p, i, n: (p, i, 0)),
                pl.BlockSpec((2, block, 1), lambda p, i, n: (p, i, 0)),
            ],
            out_specs=[
                pl.BlockSpec((block, lane), lambda p, i, n: (i, p)),
                pl.BlockSpec((seq, lane), lambda p, i, n: (0, p)),
                pl.BlockSpec((seq, lane), lambda p, i, n: (0, p)),
            ],
        ),
        compiler_params=pltpu.CompilerParams(dimension_semantics=("parallel", "arbitrary")),
        cost_estimate=pl.CostEstimate(
            flops=20 * seq * seq * width, transcendentals=seq * seq * pairs * 2,
            bytes_accessed=2 * seq * width * 2 * (2 + 2 * seq // block) + 3 * seq * width * 4,
        ),
    )(length, q, k, v, g, top, total)


def gelu_tanh(inner):
    return jax.nn.gelu(inner, approximate=True)


ALL = ("dp", "fsdp")


COLUMNS = 384
GATHER_COLUMNS = 128
PROJECT_LATE = 382


def pad_columns(blocks, multiple=COLUMNS):
    width = sum(block.shape[1] for block in blocks)
    extra = -width % multiple
    if extra:
        blocks = blocks + [jnp.zeros((blocks[0].shape[0], extra), blocks[0].dtype)]
    return jnp.concatenate(blocks, axis=1)


def split_columns(packed, widths):
    pieces = []
    offset = 0
    for width in widths:
        pieces.append(packed[:, offset : offset + width])
        offset += width
    return pieces


def gather_columns(blocks):
    packed = pad_columns(blocks, GATHER_COLUMNS)
    full = lax.all_gather(packed[None], ALL, axis=0, tiled=True)
    full = full.reshape(full.shape[0] * full.shape[1], full.shape[2])
    return split_columns(full, [block.shape[1] for block in blocks])


def scatter_columns(packed, widths):
    summed = lax.psum_scatter(packed, ALL, scatter_dimension=0, tiled=True)
    return [piece.astype(jnp.float32) for piece in split_columns(summed, widths)]


def as_column(vector, rows):
    return vector.reshape(rows, -1)


def body(
    tokens,
    lengths,
    attend_weight,
    project_weight,
    expand_weight,
    contract_weight,
    inner_bias,
    outer_bias,
    norm_gain,
    norm_shift,
    cotangent,
):
    seq_dev, seq_len, width = tokens.shape
    positions = seq_dev * seq_len
    rows_dev = attend_weight.shape[0]
    attend_full, gain_full, shift_full, inner_full, outer_full = gather_columns(
        [
            attend_weight,
            as_column(norm_gain, rows_dev),
            as_column(norm_shift, rows_dev),
            as_column(inner_bias, rows_dev),
            as_column(outer_bias, rows_dev),
        ],
    )
    gain_full = gain_full.reshape(-1)
    shift_full = shift_full.reshape(-1)
    inner_full = inner_full.reshape(-1)
    outer_full = outer_full.reshape(-1)
    expand_full, project_full = gather_columns([expand_weight, project_weight])
    (contract_full,) = gather_columns([contract_weight])
    rows = tokens.reshape(positions, width).astype(jnp.float32)
    normed, norm_pull = jax.vjp(
        layer_norm, rows, gain_full.astype(jnp.float32), shift_full.astype(jnp.float32)
    )
    normed_low = normed.astype(jnp.bfloat16)
    triple = jnp.dot(normed_low, attend_full, preferred_element_type=jnp.float32).reshape(
        seq_dev, seq_len, 3, HEADS, HEAD_DIM
    )
    cosine, sine = rotary_tables(seq_len)

    def turn(query, keys):
        return (rotate(query, cosine, sine), rotate(keys, cosine, sine))

    (query, keys), turn_pull = jax.vjp(turn, triple[:, :, 0], triple[:, :, 1])
    query_low = query.astype(jnp.bfloat16)
    keys_low = keys.astype(jnp.bfloat16)
    values_low = triple[:, :, 2].astype(jnp.bfloat16)
    flat_query = query_low.reshape(seq_dev, seq_len, width)
    flat_keys = keys_low.reshape(seq_dev, seq_len, width)
    flat_values = values_low.reshape(seq_dev, seq_len, width)
    forward_parts = [
        attention_forward(flat_query[s], flat_keys[s], flat_values[s], lengths[s : s + 1])
        for s in range(seq_dev)
    ]
    mixed_low = jnp.concatenate([part[0] for part in forward_parts], axis=0)
    hidden = jnp.dot(
        normed_low, expand_full, preferred_element_type=jnp.float32
    ) + inner_full.astype(jnp.float32)
    active, gelu_pull = jax.vjp(gelu_tanh, hidden)
    active_low = active.astype(jnp.bfloat16)
    result = rows + jnp.dot(mixed_low, project_full, preferred_element_type=jnp.float32)
    result = (
        result
        + jnp.dot(active_low, contract_full, preferred_element_type=jnp.float32)
        + outer_full.astype(jnp.float32)
    )
    output = result.astype(jnp.bfloat16).reshape(tokens.shape)
    upstream = cotangent.reshape(positions, width)
    contract_grad = jnp.einsum(
        "tf,td->fd", active_low, upstream, preferred_element_type=jnp.float32
    )
    rows_all = normed_low.shape[1]
    first = [contract_grad.astype(jnp.bfloat16)]
    first_packed = pad_columns(first)
    first_packed, upstream_back = lax.optimization_barrier((first_packed, upstream))
    (contract_part,) = scatter_columns(first_packed, [block.shape[1] for block in first])
    contract_part = contract_part.reshape(-1, width)
    outer_grad = jnp.sum(upstream_back, axis=0, dtype=jnp.float32)
    project_grad = jnp.einsum(
        "te,td->ed", mixed_low, upstream_back, preferred_element_type=jnp.float32
    )
    active_grad = jnp.einsum(
        "td,fd->tf", upstream_back, contract_full, preferred_element_type=jnp.float32
    )
    hidden_grad = gelu_pull(active_grad)[0].astype(jnp.bfloat16)
    expand_grad = jnp.einsum(
        "te,tf->ef", normed_low, hidden_grad, preferred_element_type=jnp.float32
    )
    inner_grad = jnp.sum(hidden_grad, axis=0, dtype=jnp.float32)
    early = [
        expand_grad.astype(jnp.bfloat16),
        project_grad.astype(jnp.bfloat16)[:, PROJECT_LATE:],
        as_column(inner_grad.astype(jnp.bfloat16), rows_all),
        as_column(outer_grad.astype(jnp.bfloat16), rows_all),
    ]
    early_widths = [block.shape[1] for block in early]
    early_packed = pad_columns(early)
    normed_grad = jnp.einsum(
        "tf,ef->te", hidden_grad, expand_full, preferred_element_type=jnp.float32
    )
    mixed_grad = jnp.einsum("td,ed->te", upstream, project_full, preferred_element_type=jnp.float32)
    mixed_grad = mixed_grad.astype(jnp.bfloat16).reshape(seq_dev, seq_len, width)
    early_packed, mixed_grad = lax.optimization_barrier((early_packed, mixed_grad))
    expand_part, project_part, inner_part, outer_part = scatter_columns(early_packed, early_widths)
    inner_part = inner_part.reshape(-1)
    outer_part = outer_part.reshape(-1)
    backward_parts = [
        attention_backward(
            flat_query[s],
            flat_keys[s],
            flat_values[s],
            mixed_grad[s],
            forward_parts[s][1],
            forward_parts[s][2],
            lengths[s : s + 1],
        )
        for s in range(seq_dev)
    ]
    query_grad, key_grad, value_grad = (
        jnp.stack([part[j] for part in backward_parts]).reshape(seq_dev, seq_len, HEADS, HEAD_DIM)
        for j in range(3)
    )
    query_turned, key_turned = turn_pull((query_grad, key_grad))
    triple_grad = (
        jnp.stack([query_turned, key_turned, value_grad], axis=2)
        .reshape(positions, 3 * width)
        .astype(jnp.bfloat16)
    )
    attend_grad = jnp.einsum(
        "te,tc->ec", normed_low, triple_grad, preferred_element_type=jnp.float32
    )
    normed_grad = normed_grad + jnp.einsum(
        "tc,ec->te", triple_grad, attend_full, preferred_element_type=jnp.float32
    )
    rows_grad, gain_grad, shift_grad = norm_pull(normed_grad)
    token_grad = (
        (upstream.astype(jnp.float32) + rows_grad).astype(jnp.bfloat16).reshape(tokens.shape)
    )
    late = [
        attend_grad.astype(jnp.bfloat16),
        as_column(gain_grad.astype(jnp.bfloat16), rows_all),
        as_column(shift_grad.astype(jnp.bfloat16), rows_all),
        project_grad.astype(jnp.bfloat16)[:, :PROJECT_LATE],
    ]
    attend_part, gain_part, shift_part, project_head = scatter_columns(
        pad_columns(late), [block.shape[1] for block in late]
    )
    gain_part = gain_part.reshape(-1)
    shift_part = shift_part.reshape(-1)
    project_part = jnp.concatenate([project_head, project_part], axis=1)
    return (
        output,
        token_grad,
        attend_part,
        project_part,
        expand_part,
        contract_part,
        inner_part,
        outer_part,
        gain_part,
        shift_part,
    )


def solution(mesh):
    return jax.shard_map(
        body,
        mesh=mesh,
        in_specs=(
            P(("dp", "fsdp"), None, None),
            P(("dp", "fsdp")),
            P(("dp", "fsdp"), None),
            P(("dp", "fsdp"), None),
            P(("dp", "fsdp"), None),
            P(("dp", "fsdp"), None),
            P(("dp", "fsdp")),
            P(("dp", "fsdp")),
            P(("dp", "fsdp")),
            P(("dp", "fsdp")),
            P(("dp", "fsdp"), None, None),
        ),
        out_specs=(
            P(("dp", "fsdp"), None, None),
            P(("dp", "fsdp"), None, None),
            P(("dp", "fsdp"), None),
            P(("dp", "fsdp"), None),
            P(("dp", "fsdp"), None),
            P(("dp", "fsdp"), None),
            P(("dp", "fsdp")),
            P(("dp", "fsdp")),
            P(("dp", "fsdp")),
            P(("dp", "fsdp")),
        ),
        check_vma=False,
    )
```

```python
import math

import jax
import jax.numpy as jnp
from jax import lax
from jax.experimental import pallas as pl
from jax.experimental.pallas import tpu as pltpu
from jax.sharding import PartitionSpec as P


HEADS = 16
HEAD_DIM = 64
ROT = 32


epsilon = 1e-05


def layer_norm(rows, gain, shift):
    center = jnp.mean(rows, axis=-1, keepdims=True)
    spread = rows - center
    variance = jnp.mean(spread * spread, axis=-1, keepdims=True)
    return spread * lax.rsqrt(variance + epsilon) * gain + shift


def rotary_tables(length):
    position = jnp.arange(length).astype(jnp.float32)[:, None]
    ladder = jnp.arange(ROT // 2).astype(jnp.float32) * (-2.0 * math.log(10000.0) / ROT)
    angle = position * jnp.exp(ladder)[None, :]
    return (jnp.cos(angle)[:, None, :], jnp.sin(angle)[:, None, :])


def rotate(field, cosine, sine):
    paired = field[..., :ROT].reshape(field.shape[:-1] + (ROT // 2, 2))
    first = paired[..., 0]
    second = paired[..., 1]
    turned = jnp.stack([first * cosine - second * sine, second * cosine + first * sine], axis=-1)
    return jnp.concatenate([turned.reshape(field.shape[:-1] + (ROT,)), field[..., ROT:]], axis=-1)


QUERY_BLOCK = 256
NT = (((1,), (1,)), ((), ()))
TN = (((0,), (0,)), ((), ()))


def head_scores(q, k, first, length, lane_mask):
    scores = lax.dot_general(
        jnp.where(lane_mask, q, jnp.zeros_like(q)), k, NT, preferred_element_type=jnp.float32
    ) * HEAD_DIM ** (-0.5)
    query_place = first + lax.broadcasted_iota(jnp.int32, scores.shape, 0)
    key_place = lax.broadcasted_iota(jnp.int32, scores.shape, 1)
    allowed = (key_place <= query_place) & (key_place < length)
    return jnp.where(allowed, scores, -1000000000.0)


def attention_forward_kernel(length_ref, q_ref, k_ref, v_ref, o_ref, top_ref, total_ref):
    block = q_ref.shape[0]
    first = pl.program_id(1) * block
    length = length_ref[0]
    q = q_ref[...]
    k = k_ref[...]
    v = v_ref[...]
    lanes = lax.broadcasted_iota(jnp.int32, q.shape, 1)
    result = None
    for head in range(2):
        lane_mask = (lanes >= head * HEAD_DIM) & (lanes < (head + 1) * HEAD_DIM)
        masked = head_scores(q, k, first, length, lane_mask)
        top = jnp.max(masked, axis=-1, keepdims=True)
        weights = jnp.exp(masked - top)
        total = jnp.sum(weights, axis=-1, keepdims=True)
        probs = (weights / total).astype(jnp.bfloat16)
        out = jnp.dot(probs, v, preferred_element_type=jnp.float32)
        result = out if result is None else jnp.where(lane_mask, out, result)
        top_ref[head] = top
        total_ref[head] = total
    o_ref[...] = result.astype(o_ref.dtype)


def attention_backward_kernel(
    length_ref, q_ref, k_ref, v_ref, g_ref, top_ref, total_ref, dq_ref, dk_ref, dv_ref
):
    block = q_ref.shape[0]
    step = pl.program_id(1)
    first = step * block
    length = length_ref[0]
    scale = HEAD_DIM ** (-0.5)

    @pl.when(step == 0)
    def _():
        dk_ref[...] = jnp.zeros_like(dk_ref)
        dv_ref[...] = jnp.zeros_like(dv_ref)

    q = q_ref[...]
    k = k_ref[...]
    v = v_ref[...]
    g = g_ref[...]
    lanes = lax.broadcasted_iota(jnp.int32, q.shape, 1)
    key_lanes = lax.broadcasted_iota(jnp.int32, k.shape, 1)
    dq = None
    dk = None
    dv = None
    for head in range(2):
        lane_mask = (lanes >= head * HEAD_DIM) & (lanes < (head + 1) * HEAD_DIM)
        key_mask = (key_lanes >= head * HEAD_DIM) & (key_lanes < (head + 1) * HEAD_DIM)
        masked = head_scores(q, k, first, length, lane_mask)
        probs = jnp.exp(masked - top_ref[head]) / total_ref[head]
        upward = lax.dot_general(
            jnp.where(lane_mask, g, jnp.zeros_like(g)), v, NT, preferred_element_type=jnp.float32
        )
        inner = jnp.sum(probs * upward, axis=-1, keepdims=True)
        score_grad = (probs * (upward - inner)).astype(jnp.bfloat16)
        dq_head = jnp.dot(score_grad, k, preferred_element_type=jnp.float32) * scale
        dk_head = lax.dot_general(score_grad, q, TN, preferred_element_type=jnp.float32) * scale
        dv_head = lax.dot_general(
            probs.astype(jnp.bfloat16), g, TN, preferred_element_type=jnp.float32
        )
        if dq is None:
            dq, dk, dv = dq_head, dk_head, dv_head
        else:
            dq = jnp.where(lane_mask, dq_head, dq)
            dk = jnp.where(key_mask, dk_head, dk)
            dv = jnp.where(key_mask, dv_head, dv)
    dq_ref[...] = dq
    dk_ref[...] += dk
    dv_ref[...] += dv


def attention_forward(q, k, v, length):
    seq, width = q.shape
    pairs = width // (2 * HEAD_DIM)
    block = min(QUERY_BLOCK, seq)
    grid = (pairs, seq // block)
    lane = 2 * HEAD_DIM
    return pl.pallas_call(
        attention_forward_kernel,
        out_shape=(
            jax.ShapeDtypeStruct((seq, width), jnp.bfloat16),
            jax.ShapeDtypeStruct((2 * pairs, seq, 1), jnp.float32),
            jax.ShapeDtypeStruct((2 * pairs, seq, 1), jnp.float32),
        ),
        grid_spec=pltpu.PrefetchScalarGridSpec(
            num_scalar_prefetch=1,
            grid=grid,
            in_specs=[
                pl.BlockSpec((block, lane), lambda p, i, n: (i, p)),
                pl.BlockSpec((seq, lane), lambda p, i, n: (0, p)),
                pl.BlockSpec((seq, lane), lambda p, i, n: (0, p)),
            ],
            out_specs=[
                pl.BlockSpec((block, lane), lambda p, i, n: (i, p)),
                pl.BlockSpec((2, block, 1), lambda p, i, n: (p, i, 0)),
                pl.BlockSpec((2, block, 1), lambda p, i, n: (p, i, 0)),
            ],
        ),
        compiler_params=pltpu.CompilerParams(dimension_semantics=("parallel", "arbitrary")),
        cost_estimate=pl.CostEstimate(
            flops=8 * seq * seq * width, transcendentals=seq * seq * pairs * 2,
            bytes_accessed=2 * seq * width * 2 * (1 + 2 * seq // block),
        ),
    )(length, q, k, v)


def attention_backward(q, k, v, g, top, total, length):
    seq, width = q.shape
    pairs = width // (2 * HEAD_DIM)
    block = min(QUERY_BLOCK, seq)
    grid = (pairs, seq // block)
    lane = 2 * HEAD_DIM
    return pl.pallas_call(
        attention_backward_kernel,
        out_shape=(
            jax.ShapeDtypeStruct((seq, width), jnp.float32),
            jax.ShapeDtypeStruct((seq, width), jnp.float32),
            jax.ShapeDtypeStruct((seq, width), jnp.float32),
        ),
        grid_spec=pltpu.PrefetchScalarGridSpec(
            num_scalar_prefetch=1,
            grid=grid,
            in_specs=[
                pl.BlockSpec((block, lane), lambda p, i, n: (i, p)),
                pl.BlockSpec((seq, lane), lambda p, i, n: (0, p)),
                pl.BlockSpec((seq, lane), lambda p, i, n: (0, p)),
                pl.BlockSpec((block, lane), lambda p, i, n: (i, p)),
                pl.BlockSpec((2, block, 1), lambda p, i, n: (p, i, 0)),
                pl.BlockSpec((2, block, 1), lambda p, i, n: (p, i, 0)),
            ],
            out_specs=[
                pl.BlockSpec((block, lane), lambda p, i, n: (i, p)),
                pl.BlockSpec((seq, lane), lambda p, i, n: (0, p)),
                pl.BlockSpec((seq, lane), lambda p, i, n: (0, p)),
            ],
        ),
        compiler_params=pltpu.CompilerParams(dimension_semantics=("parallel", "arbitrary")),
        cost_estimate=pl.CostEstimate(
            flops=20 * seq * seq * width, transcendentals=seq * seq * pairs * 2,
            bytes_accessed=2 * seq * width * 2 * (2 + 2 * seq // block) + 3 * seq * width * 4,
        ),
    )(length, q, k, v, g, top, total)


def gelu_tanh(inner):
    return jax.nn.gelu(inner, approximate=True)


ALL = ("dp", "fsdp")


COLUMNS = 384
GATHER_COLUMNS = 128
PROJECT_LATE = 382


def pad_columns(blocks, multiple=COLUMNS):
    width = sum(block.shape[1] for block in blocks)
    extra = -width % multiple
    if extra:
        blocks = blocks + [jnp.zeros((blocks[0].shape[0], extra), blocks[0].dtype)]
    return jnp.concatenate(blocks, axis=1)


def split_columns(packed, widths):
    pieces = []
    offset = 0
    for width in widths:
        pieces.append(packed[:, offset : offset + width])
        offset += width
    return pieces


def gather_columns(blocks):
    packed = pad_columns(blocks, GATHER_COLUMNS)
    full = lax.all_gather(packed[None], ALL, axis=0, tiled=True)
    full = full.reshape(full.shape[0] * full.shape[1], full.shape[2])
    return split_columns(full, [block.shape[1] for block in blocks])


def scatter_columns(packed, widths):
    summed = lax.psum_scatter(packed, ALL, scatter_dimension=0, tiled=True)
    return [piece.astype(jnp.float32) for piece in split_columns(summed, widths)]


def as_column(vector, rows):
    return vector.reshape(rows, -1)


def body(
    tokens,
    lengths,
    attend_weight,
    project_weight,
    expand_weight,
    contract_weight,
    inner_bias,
    outer_bias,
    norm_gain,
    norm_shift,
    cotangent,
):
    seq_dev, seq_len, width = tokens.shape
    positions = seq_dev * seq_len
    rows_dev = attend_weight.shape[0]
    attend_full, gain_full, shift_full, inner_full, outer_full = gather_columns(
        [
            attend_weight,
            as_column(norm_gain, rows_dev),
            as_column(norm_shift, rows_dev),
            as_column(inner_bias, rows_dev),
            as_column(outer_bias, rows_dev),
        ],
    )
    gain_full = gain_full.reshape(-1)
    shift_full = shift_full.reshape(-1)
    inner_full = inner_full.reshape(-1)
    outer_full = outer_full.reshape(-1)
    expand_full, project_full = gather_columns([expand_weight, project_weight])
    (contract_full,) = gather_columns([contract_weight])
    rows = tokens.reshape(positions, width).astype(jnp.float32)
    normed, norm_pull = jax.vjp(
        layer_norm, rows, gain_full.astype(jnp.float32), shift_full.astype(jnp.float32)
    )
    normed_low = normed.astype(jnp.bfloat16)
    triple = jnp.dot(normed_low, attend_full, preferred_element_type=jnp.float32).reshape(
        seq_dev, seq_len, 3, HEADS, HEAD_DIM
    )
    cosine, sine = rotary_tables(seq_len)

    def turn(query, keys):
        return (rotate(query, cosine, sine), rotate(keys, cosine, sine))

    (query, keys), turn_pull = jax.vjp(turn, triple[:, :, 0], triple[:, :, 1])
    query_low = query.astype(jnp.bfloat16)
    keys_low = keys.astype(jnp.bfloat16)
    values_low = triple[:, :, 2].astype(jnp.bfloat16)
    flat_query = query_low.reshape(seq_dev, seq_len, width)
    flat_keys = keys_low.reshape(seq_dev, seq_len, width)
    flat_values = values_low.reshape(seq_dev, seq_len, width)
    forward_parts = [
        attention_forward(flat_query[s], flat_keys[s], flat_values[s], lengths[s : s + 1])
        for s in range(seq_dev)
    ]
    mixed_low = jnp.concatenate([part[0] for part in forward_parts], axis=0)
    hidden = jnp.dot(
        normed_low, expand_full, preferred_element_type=jnp.float32
    ) + inner_full.astype(jnp.float32)
    active, gelu_pull = jax.vjp(gelu_tanh, hidden)
    active_low = active.astype(jnp.bfloat16)
    result = rows + jnp.dot(mixed_low, project_full, preferred_element_type=jnp.float32)
    result = (
        result
        + jnp.dot(active_low, contract_full, preferred_element_type=jnp.float32)
        + outer_full.astype(jnp.float32)
    )
    output = result.astype(jnp.bfloat16).reshape(tokens.shape)
    upstream = cotangent.reshape(positions, width)
    contract_grad = jnp.einsum(
        "tf,td->fd", active_low, upstream, preferred_element_type=jnp.float32
    )
    rows_all = normed_low.shape[1]
    project_grad = jnp.einsum(
        "te,td->ed", mixed_low, upstream, preferred_element_type=jnp.float32
    ).astype(jnp.bfloat16)
    ratio = contract_grad.shape[0] // rows_all
    quarter = width // ratio
    spare = -width % COLUMNS
    project_rows = project_grad.reshape(ratio * rows_all, quarter)
    project_rest = project_grad.reshape(rows_all, ratio, quarter)[:, :, : quarter - spare]
    project_rest = project_rest.reshape(rows_all, -1)
    first = [contract_grad.astype(jnp.bfloat16), project_rows[:, quarter - spare :]]
    first_packed = pad_columns(first)
    first_packed, upstream_back = lax.optimization_barrier((first_packed, upstream))
    contract_part, project_tail = scatter_columns(first_packed, [block.shape[1] for block in first])
    contract_part = contract_part.reshape(-1, width)
    outer_grad = jnp.sum(upstream_back, axis=0, dtype=jnp.float32)
    active_grad = jnp.einsum(
        "td,fd->tf", upstream_back, contract_full, preferred_element_type=jnp.float32
    )
    hidden_grad = gelu_pull(active_grad)[0].astype(jnp.bfloat16)
    expand_grad = jnp.einsum(
        "te,tf->ef", normed_low, hidden_grad, preferred_element_type=jnp.float32
    )
    inner_grad = jnp.sum(hidden_grad, axis=0, dtype=jnp.float32)
    early = [
        expand_grad.astype(jnp.bfloat16),
        project_rest[:, PROJECT_LATE:],
        as_column(inner_grad.astype(jnp.bfloat16), rows_all),
        as_column(outer_grad.astype(jnp.bfloat16), rows_all),
    ]
    early_widths = [block.shape[1] for block in early]
    early_packed = pad_columns(early)
    normed_grad = jnp.einsum(
        "tf,ef->te", hidden_grad, expand_full, preferred_element_type=jnp.float32
    )
    mixed_grad = jnp.einsum("td,ed->te", upstream, project_full, preferred_element_type=jnp.float32)
    mixed_grad = mixed_grad.astype(jnp.bfloat16).reshape(seq_dev, seq_len, width)
    early_packed, mixed_grad = lax.optimization_barrier((early_packed, mixed_grad))
    expand_part, project_part, inner_part, outer_part = scatter_columns(early_packed, early_widths)
    inner_part = inner_part.reshape(-1)
    outer_part = outer_part.reshape(-1)
    backward_parts = [
        attention_backward(
            flat_query[s],
            flat_keys[s],
            flat_values[s],
            mixed_grad[s],
            forward_parts[s][1],
            forward_parts[s][2],
            lengths[s : s + 1],
        )
        for s in range(seq_dev)
    ]
    query_grad, key_grad, value_grad = (
        jnp.stack([part[j] for part in backward_parts]).reshape(seq_dev, seq_len, HEADS, HEAD_DIM)
        for j in range(3)
    )
    query_turned, key_turned = turn_pull((query_grad, key_grad))
    triple_grad = (
        jnp.stack([query_turned, key_turned, value_grad], axis=2)
        .reshape(positions, 3 * width)
        .astype(jnp.bfloat16)
    )
    attend_grad = jnp.einsum(
        "te,tc->ec", normed_low, triple_grad, preferred_element_type=jnp.float32
    )
    normed_grad = normed_grad + jnp.einsum(
        "tc,ec->te", triple_grad, attend_full, preferred_element_type=jnp.float32
    )
    rows_grad, gain_grad, shift_grad = norm_pull(normed_grad)
    token_grad = (
        (upstream.astype(jnp.float32) + rows_grad).astype(jnp.bfloat16).reshape(tokens.shape)
    )
    late = [
        attend_grad.astype(jnp.bfloat16),
        as_column(gain_grad.astype(jnp.bfloat16), rows_all),
        as_column(shift_grad.astype(jnp.bfloat16), rows_all),
        project_rest[:, :PROJECT_LATE],
    ]
    attend_part, gain_part, shift_part, project_head = scatter_columns(
        pad_columns(late), [block.shape[1] for block in late]
    )
    gain_part = gain_part.reshape(-1)
    shift_part = shift_part.reshape(-1)
    rows_dev_out = project_head.shape[0]
    project_front = jnp.concatenate([project_head, project_part], axis=1).reshape(
        rows_dev_out, ratio, quarter - spare
    )
    project_back = project_tail.reshape(rows_dev_out, ratio, spare)
    project_part = jnp.concatenate([project_front, project_back], axis=2).reshape(
        rows_dev_out, width
    )
    return (
        output,
        token_grad,
        attend_part,
        project_part,
        expand_part,
        contract_part,
        inner_part,
        outer_part,
        gain_part,
        shift_part,
    )


def solution(mesh):
    return jax.shard_map(
        body,
        mesh=mesh,
        in_specs=(
            P(("dp", "fsdp"), None, None),
            P(("dp", "fsdp")),
            P(("dp", "fsdp"), None),
            P(("dp", "fsdp"), None),
            P(("dp", "fsdp"), None),
            P(("dp", "fsdp"), None),
            P(("dp", "fsdp")),
            P(("dp", "fsdp")),
            P(("dp", "fsdp")),
            P(("dp", "fsdp")),
            P(("dp", "fsdp"), None, None),
        ),
        out_specs=(
            P(("dp", "fsdp"), None, None),
            P(("dp", "fsdp"), None, None),
            P(("dp", "fsdp"), None),
            P(("dp", "fsdp"), None),
            P(("dp", "fsdp"), None),
            P(("dp", "fsdp"), None),
            P(("dp", "fsdp")),
            P(("dp", "fsdp")),
            P(("dp", "fsdp")),
            P(("dp", "fsdp")),
        ),
        check_vma=False,
    )
```

```python
import math

import jax
import jax.numpy as jnp
from jax import lax
from jax.experimental import pallas as pl
from jax.experimental.pallas import tpu as pltpu
from jax.sharding import PartitionSpec as P


HEADS = 16
HEAD_DIM = 64
ROT = 32


epsilon = 1e-05


def layer_norm(rows, gain, shift):
    center = jnp.mean(rows, axis=-1, keepdims=True)
    spread = rows - center
    variance = jnp.mean(spread * spread, axis=-1, keepdims=True)
    return spread * lax.rsqrt(variance + epsilon) * gain + shift


def rotary_tables(length):
    position = jnp.arange(length).astype(jnp.float32)[:, None]
    ladder = jnp.arange(ROT // 2).astype(jnp.float32) * (-2.0 * math.log(10000.0) / ROT)
    angle = position * jnp.exp(ladder)[None, :]
    return (jnp.cos(angle)[:, None, :], jnp.sin(angle)[:, None, :])


def rotate(field, cosine, sine):
    paired = field[..., :ROT].reshape(field.shape[:-1] + (ROT // 2, 2))
    first = paired[..., 0]
    second = paired[..., 1]
    turned = jnp.stack([first * cosine - second * sine, second * cosine + first * sine], axis=-1)
    return jnp.concatenate([turned.reshape(field.shape[:-1] + (ROT,)), field[..., ROT:]], axis=-1)


QUERY_BLOCK = 256
NT = (((1,), (1,)), ((), ()))
TN = (((0,), (0,)), ((), ()))


def head_scores(q, k, first, length, lane_mask):
    scores = lax.dot_general(
        jnp.where(lane_mask, q, jnp.zeros_like(q)), k, NT, preferred_element_type=jnp.float32
    ) * HEAD_DIM ** (-0.5)
    query_place = first + lax.broadcasted_iota(jnp.int32, scores.shape, 0)
    key_place = lax.broadcasted_iota(jnp.int32, scores.shape, 1)
    allowed = (key_place <= query_place) & (key_place < length)
    return jnp.where(allowed, scores, -1000000000.0)


def attention_forward_kernel(length_ref, q_ref, k_ref, v_ref, o_ref, top_ref, total_ref):
    block = q_ref.shape[0]
    first = pl.program_id(1) * block
    length = length_ref[0]
    q = q_ref[...]
    k = k_ref[...]
    v = v_ref[...]
    lanes = lax.broadcasted_iota(jnp.int32, q.shape, 1)
    result = None
    for head in range(2):
        lane_mask = (lanes >= head * HEAD_DIM) & (lanes < (head + 1) * HEAD_DIM)
        masked = head_scores(q, k, first, length, lane_mask)
        top = jnp.max(masked, axis=-1, keepdims=True)
        weights = jnp.exp(masked - top)
        total = jnp.sum(weights, axis=-1, keepdims=True)
        probs = (weights / total).astype(jnp.bfloat16)
        out = jnp.dot(probs, v, preferred_element_type=jnp.float32)
        result = out if result is None else jnp.where(lane_mask, out, result)
        top_ref[head] = top
        total_ref[head] = total
    o_ref[...] = result.astype(o_ref.dtype)


def attention_backward_kernel(
    length_ref, q_ref, k_ref, v_ref, g_ref, top_ref, total_ref, dq_ref, dk_ref, dv_ref
):
    block = q_ref.shape[0]
    step = pl.program_id(1)
    first = step * block
    length = length_ref[0]
    scale = HEAD_DIM ** (-0.5)

    @pl.when(step == 0)
    def _():
        dk_ref[...] = jnp.zeros_like(dk_ref)
        dv_ref[...] = jnp.zeros_like(dv_ref)

    q = q_ref[...]
    k = k_ref[...]
    v = v_ref[...]
    g = g_ref[...]
    lanes = lax.broadcasted_iota(jnp.int32, q.shape, 1)
    key_lanes = lax.broadcasted_iota(jnp.int32, k.shape, 1)
    dq = None
    dk = None
    dv = None
    for head in range(2):
        lane_mask = (lanes >= head * HEAD_DIM) & (lanes < (head + 1) * HEAD_DIM)
        key_mask = (key_lanes >= head * HEAD_DIM) & (key_lanes < (head + 1) * HEAD_DIM)
        masked = head_scores(q, k, first, length, lane_mask)
        probs = jnp.exp(masked - top_ref[head]) / total_ref[head]
        upward = lax.dot_general(
            jnp.where(lane_mask, g, jnp.zeros_like(g)), v, NT, preferred_element_type=jnp.float32
        )
        inner = jnp.sum(probs * upward, axis=-1, keepdims=True)
        score_grad = (probs * (upward - inner)).astype(jnp.bfloat16)
        dq_head = jnp.dot(score_grad, k, preferred_element_type=jnp.float32) * scale
        dk_head = lax.dot_general(score_grad, q, TN, preferred_element_type=jnp.float32) * scale
        dv_head = lax.dot_general(
            probs.astype(jnp.bfloat16), g, TN, preferred_element_type=jnp.float32
        )
        if dq is None:
            dq, dk, dv = dq_head, dk_head, dv_head
        else:
            dq = jnp.where(lane_mask, dq_head, dq)
            dk = jnp.where(key_mask, dk_head, dk)
            dv = jnp.where(key_mask, dv_head, dv)
    dq_ref[...] = dq
    dk_ref[...] += dk
    dv_ref[...] += dv


def attention_forward(q, k, v, length):
    seq, width = q.shape
    pairs = width // (2 * HEAD_DIM)
    block = min(QUERY_BLOCK, seq)
    grid = (pairs, seq // block)
    lane = 2 * HEAD_DIM
    return pl.pallas_call(
        attention_forward_kernel,
        out_shape=(
            jax.ShapeDtypeStruct((seq, width), jnp.bfloat16),
            jax.ShapeDtypeStruct((2 * pairs, seq, 1), jnp.float32),
            jax.ShapeDtypeStruct((2 * pairs, seq, 1), jnp.float32),
        ),
        grid_spec=pltpu.PrefetchScalarGridSpec(
            num_scalar_prefetch=1,
            grid=grid,
            in_specs=[
                pl.BlockSpec((block, lane), lambda p, i, n: (i, p)),
                pl.BlockSpec((seq, lane), lambda p, i, n: (0, p)),
                pl.BlockSpec((seq, lane), lambda p, i, n: (0, p)),
            ],
            out_specs=[
                pl.BlockSpec((block, lane), lambda p, i, n: (i, p)),
                pl.BlockSpec((2, block, 1), lambda p, i, n: (p, i, 0)),
                pl.BlockSpec((2, block, 1), lambda p, i, n: (p, i, 0)),
            ],
        ),
        compiler_params=pltpu.CompilerParams(dimension_semantics=("parallel", "arbitrary")),
        cost_estimate=pl.CostEstimate(
            flops=8 * seq * seq * width, transcendentals=seq * seq * pairs * 2,
            bytes_accessed=2 * seq * width * 2 * (1 + 2 * seq // block),
        ),
    )(length, q, k, v)


def attention_backward(q, k, v, g, top, total, length):
    seq, width = q.shape
    pairs = width // (2 * HEAD_DIM)
    block = min(QUERY_BLOCK, seq)
    grid = (pairs, seq // block)
    lane = 2 * HEAD_DIM
    return pl.pallas_call(
        attention_backward_kernel,
        out_shape=(
            jax.ShapeDtypeStruct((seq, width), jnp.float32),
            jax.ShapeDtypeStruct((seq, width), jnp.float32),
            jax.ShapeDtypeStruct((seq, width), jnp.float32),
        ),
        grid_spec=pltpu.PrefetchScalarGridSpec(
            num_scalar_prefetch=1,
            grid=grid,
            in_specs=[
                pl.BlockSpec((block, lane), lambda p, i, n: (i, p)),
                pl.BlockSpec((seq, lane), lambda p, i, n: (0, p)),
                pl.BlockSpec((seq, lane), lambda p, i, n: (0, p)),
                pl.BlockSpec((block, lane), lambda p, i, n: (i, p)),
                pl.BlockSpec((2, block, 1), lambda p, i, n: (p, i, 0)),
                pl.BlockSpec((2, block, 1), lambda p, i, n: (p, i, 0)),
            ],
            out_specs=[
                pl.BlockSpec((block, lane), lambda p, i, n: (i, p)),
                pl.BlockSpec((seq, lane), lambda p, i, n: (0, p)),
                pl.BlockSpec((seq, lane), lambda p, i, n: (0, p)),
            ],
        ),
        compiler_params=pltpu.CompilerParams(dimension_semantics=("parallel", "arbitrary")),
        cost_estimate=pl.CostEstimate(
            flops=20 * seq * seq * width, transcendentals=seq * seq * pairs * 2,
            bytes_accessed=2 * seq * width * 2 * (2 + 2 * seq // block) + 3 * seq * width * 4,
        ),
    )(length, q, k, v, g, top, total)


def gelu_tanh(inner):
    return jax.nn.gelu(inner, approximate=True)


ALL = ("dp", "fsdp")


COLUMNS = 384
GATHER_COLUMNS = 128
PROJECT_LATE = 382


def pad_columns(blocks, multiple=COLUMNS):
    width = sum(block.shape[1] for block in blocks)
    extra = -width % multiple
    if extra:
        blocks = blocks + [jnp.zeros((blocks[0].shape[0], extra), blocks[0].dtype)]
    return jnp.concatenate(blocks, axis=1)


def split_columns(packed, widths):
    pieces = []
    offset = 0
    for width in widths:
        pieces.append(packed[:, offset : offset + width])
        offset += width
    return pieces


def gather_columns(blocks):
    packed = pad_columns(blocks, GATHER_COLUMNS)
    full = lax.all_gather(packed[None], ALL, axis=0, tiled=True)
    full = full.reshape(full.shape[0] * full.shape[1], full.shape[2])
    return split_columns(full, [block.shape[1] for block in blocks])


def scatter_columns(packed, widths):
    summed = lax.psum_scatter(packed, ALL, scatter_dimension=0, tiled=True)
    return [piece.astype(jnp.float32) for piece in split_columns(summed, widths)]


def as_column(vector, rows):
    return vector.reshape(rows, -1)


def body(
    tokens,
    lengths,
    attend_weight,
    project_weight,
    expand_weight,
    contract_weight,
    inner_bias,
    outer_bias,
    norm_gain,
    norm_shift,
    cotangent,
):
    seq_dev, seq_len, width = tokens.shape
    positions = seq_dev * seq_len
    rows_dev = attend_weight.shape[0]
    attend_full, gain_full, shift_full, inner_full, outer_full = gather_columns(
        [
            attend_weight,
            as_column(norm_gain, rows_dev),
            as_column(norm_shift, rows_dev),
            as_column(inner_bias, rows_dev),
            as_column(outer_bias, rows_dev),
        ],
    )
    gain_full = gain_full.reshape(-1)
    shift_full = shift_full.reshape(-1)
    inner_full = inner_full.reshape(-1)
    outer_full = outer_full.reshape(-1)
    expand_full, project_full, contract_raw = gather_columns(
        [expand_weight, project_weight, contract_weight.reshape(rows_dev, -1)]
    )
    rows = tokens.reshape(positions, width).astype(jnp.float32)
    normed, norm_pull = jax.vjp(
        layer_norm, rows, gain_full.astype(jnp.float32), shift_full.astype(jnp.float32)
    )
    normed_low = normed.astype(jnp.bfloat16)
    triple = jnp.dot(normed_low, attend_full, preferred_element_type=jnp.float32).reshape(
        seq_dev, seq_len, 3, HEADS, HEAD_DIM
    )
    cosine, sine = rotary_tables(seq_len)

    def turn(query, keys):
        return (rotate(query, cosine, sine), rotate(keys, cosine, sine))

    (query, keys), turn_pull = jax.vjp(turn, triple[:, :, 0], triple[:, :, 1])
    query_low = query.astype(jnp.bfloat16)
    keys_low = keys.astype(jnp.bfloat16)
    values_low = triple[:, :, 2].astype(jnp.bfloat16)
    flat_query = query_low.reshape(seq_dev, seq_len, width)
    flat_keys = keys_low.reshape(seq_dev, seq_len, width)
    flat_values = values_low.reshape(seq_dev, seq_len, width)
    forward_parts = [
        attention_forward(flat_query[s], flat_keys[s], flat_values[s], lengths[s : s + 1])
        for s in range(seq_dev)
    ]
    mixed_low = jnp.concatenate([part[0] for part in forward_parts], axis=0)
    hidden = jnp.dot(
        normed_low, expand_full, preferred_element_type=jnp.float32
    ) + inner_full.astype(jnp.float32)
    active, gelu_pull = jax.vjp(gelu_tanh, hidden)
    active_low = active.astype(jnp.bfloat16)
    upstream = cotangent.reshape(positions, width)
    contract_grad = jnp.einsum(
        "tf,td->fd", active_low, upstream, preferred_element_type=jnp.float32
    )
    rows_all = normed_low.shape[1]
    first = [contract_grad.astype(jnp.bfloat16)]
    first_packed = pad_columns(first)
    first_packed, upstream_back, contract_raw = lax.optimization_barrier(
        (first_packed, upstream, contract_raw)
    )
    contract_full = contract_raw.reshape(-1, width)
    result = rows + jnp.dot(mixed_low, project_full, preferred_element_type=jnp.float32)
    result = (
        result
        + jnp.dot(active_low, contract_full, preferred_element_type=jnp.float32)
        + outer_full.astype(jnp.float32)
    )
    output = result.astype(jnp.bfloat16).reshape(tokens.shape)
    (contract_part,) = scatter_columns(first_packed, [block.shape[1] for block in first])
    contract_part = contract_part.reshape(-1, width)
    outer_grad = jnp.sum(upstream_back, axis=0, dtype=jnp.float32)
    project_grad = jnp.einsum(
        "te,td->ed", mixed_low, upstream_back, preferred_element_type=jnp.float32
    )
    active_grad = jnp.einsum(
        "td,fd->tf", upstream_back, contract_full, preferred_element_type=jnp.float32
    )
    hidden_grad = gelu_pull(active_grad)[0].astype(jnp.bfloat16)
    expand_grad = jnp.einsum(
        "te,tf->ef", normed_low, hidden_grad, preferred_element_type=jnp.float32
    )
    inner_grad = jnp.sum(hidden_grad, axis=0, dtype=jnp.float32)
    early = [
        expand_grad.astype(jnp.bfloat16),
        project_grad.astype(jnp.bfloat16)[:, PROJECT_LATE:],
        as_column(inner_grad.astype(jnp.bfloat16), rows_all),
        as_column(outer_grad.astype(jnp.bfloat16), rows_all),
    ]
    early_widths = [block.shape[1] for block in early]
    early_packed = pad_columns(early)
    normed_grad = jnp.einsum(
        "tf,ef->te", hidden_grad, expand_full, preferred_element_type=jnp.float32
    )
    mixed_grad = jnp.einsum("td,ed->te", upstream, project_full, preferred_element_type=jnp.float32)
    mixed_grad = mixed_grad.astype(jnp.bfloat16).reshape(seq_dev, seq_len, width)
    early_packed, mixed_grad = lax.optimization_barrier((early_packed, mixed_grad))
    expand_part, project_part, inner_part, outer_part = scatter_columns(early_packed, early_widths)
    inner_part = inner_part.reshape(-1)
    outer_part = outer_part.reshape(-1)
    backward_parts = [
        attention_backward(
            flat_query[s],
            flat_keys[s],
            flat_values[s],
            mixed_grad[s],
            forward_parts[s][1],
            forward_parts[s][2],
            lengths[s : s + 1],
        )
        for s in range(seq_dev)
    ]
    query_grad, key_grad, value_grad = (
        jnp.stack([part[j] for part in backward_parts]).reshape(seq_dev, seq_len, HEADS, HEAD_DIM)
        for j in range(3)
    )
    query_turned, key_turned = turn_pull((query_grad, key_grad))
    triple_grad = (
        jnp.stack([query_turned, key_turned, value_grad], axis=2)
        .reshape(positions, 3 * width)
        .astype(jnp.bfloat16)
    )
    attend_grad = jnp.einsum(
        "te,tc->ec", normed_low, triple_grad, preferred_element_type=jnp.float32
    )
    normed_grad = normed_grad + jnp.einsum(
        "tc,ec->te", triple_grad, attend_full, preferred_element_type=jnp.float32
    )
    rows_grad, gain_grad, shift_grad = norm_pull(normed_grad)
    token_grad = (
        (upstream.astype(jnp.float32) + rows_grad).astype(jnp.bfloat16).reshape(tokens.shape)
    )
    late = [
        attend_grad.astype(jnp.bfloat16),
        as_column(gain_grad.astype(jnp.bfloat16), rows_all),
        as_column(shift_grad.astype(jnp.bfloat16), rows_all),
        project_grad.astype(jnp.bfloat16)[:, :PROJECT_LATE],
    ]
    attend_part, gain_part, shift_part, project_head = scatter_columns(
        pad_columns(late), [block.shape[1] for block in late]
    )
    gain_part = gain_part.reshape(-1)
    shift_part = shift_part.reshape(-1)
    project_part = jnp.concatenate([project_head, project_part], axis=1)
    return (
        output,
        token_grad,
        attend_part,
        project_part,
        expand_part,
        contract_part,
        inner_part,
        outer_part,
        gain_part,
        shift_part,
    )


def solution(mesh):
    return jax.shard_map(
        body,
        mesh=mesh,
        in_specs=(
            P(("dp", "fsdp"), None, None),
            P(("dp", "fsdp")),
            P(("dp", "fsdp"), None),
            P(("dp", "fsdp"), None),
            P(("dp", "fsdp"), None),
            P(("dp", "fsdp"), None),
            P(("dp", "fsdp")),
            P(("dp", "fsdp")),
            P(("dp", "fsdp")),
            P(("dp", "fsdp")),
            P(("dp", "fsdp"), None, None),
        ),
        out_specs=(
            P(("dp", "fsdp"), None, None),
            P(("dp", "fsdp"), None, None),
            P(("dp", "fsdp"), None),
            P(("dp", "fsdp"), None),
            P(("dp", "fsdp"), None),
            P(("dp", "fsdp"), None),
            P(("dp", "fsdp")),
            P(("dp", "fsdp")),
            P(("dp", "fsdp")),
            P(("dp", "fsdp")),
        ),
        check_vma=False,
    )
```
